512 devices in a mesh: param: 32 (over y_lo, z), row: 4 (over x), col: 4 (over y_hi, core).
Axes of the slice: x: 4, y: 4 (y_hi: 2, y_lo: 2; y = y_hi * 2 + y_lo), z: 16, core: 2. Of those that a mesh axis runs over, the one named last changes fastest.
Arguments:
- coefficients: bfloat16 [3, 2, 32, 512], P(None, None, 'row', 'col'), may hold values from -6 to 6
- noise_sigma: float32 [2, 32, 512], P(None, 'row', 'col'), may hold values from 0.5 to 4
- residual: float32 [2, 32, 512], P(None, 'row', 'col'), may hold values from -0.6 to 0.6
- crack_mask: int32 [32, 4], P('row', 'col'), may hold values 0 or 1
- node_panel: bfloat16 [4, 64, 3, 2048], P('row', 'col', None, 'param'), may hold values from -0.41992188 to 0.41992188
Outputs:
- hessian: float32 [2048, 2048], P('param', ('row', 'col'))
- gradient: float32 [2048], P(('param', 'row', 'col'))
The draws below stay inside these ranges and needn't reach their ends.
All inputs are finite; a program needn't handle non-finite values. No bound on the sum of `crack_mask` on one device may be relied on, other than what follows from the above.
Results may differ from the reference program's by a relative error of at most 0.0055.
Values may be sent and summed in bfloat16 or wider, within the bound.
No kernel may reach another device: no remote copies, remote signals or barrier semaphores. Data moves between devices by JAX's collectives and lax.ppermute only.
A program may use at most 64 MiB of HBM per device.

```python
import math
import jax
import jax.numpy as jnp
from jax import lax

P_SIZE = 2048
EL = 8
CAMS = 2
NROWS = 32
NCOLS = 512
NR = 4
NC = 64


def set_ends(entries, own_key, low, largest):
    extent = entries.shape
    place = [jax.random.randint(jax.random.fold_in(own_key, axis), (), 0, extent[axis]) for axis in range(len(extent))]
    entries = entries.at[tuple(place)].set(low)
    longest = extent.index(max(extent))
    place[longest] = (place[longest] + 1) % extent[longest]
    return entries.at[tuple(place)].set(largest)


def levels(rng, shape, pieces, smallest, high):
    def one(dim, parts):
        draws = jax.random.uniform(jax.random.fold_in(jax.random.fold_in(rng, 6), dim), (parts,), jnp.float32, smallest / len(pieces), high / len(pieces))
        return jnp.repeat(jnp.exp(draws), shape[dim] // parts).reshape((-1,) + (1,) * (len(shape) - dim - 1))

    level = one(*pieces[0])
    for cut in pieces[1:]:
        level = level * one(*cut)
    return level


def noise(own_key, extent, width, limit, split=(), kind=jnp.bfloat16):
    array = width * jax.random.normal(own_key, extent, jnp.float32)
    if split:
        array = array * levels(own_key, extent, split, -0.22, 0.18)
    return jnp.clip(array, -limit, limit).astype(kind)


def setup_inputs(seed: int = 0) -> dict:
    splits = jax.random.split(jax.random.key(seed), 6)
    coefficients = noise(splits[0], (3, CAMS, NROWS, NCOLS), 1.0, 6.0, ((2, 4), (3, 4)))
    noise_sigma = jnp.clip(jnp.exp(math.log(4.0) - 2.0794415 * jax.random.uniform(splits[1], (CAMS, NROWS, NCOLS), jnp.float32) ** levels(splits[1], (CAMS, NROWS, NCOLS), ((1, 4), (2, 4)), -0.2, 0.2)), 0.5, 4.0)
    residual = noise(splits[2], (CAMS, NROWS, NCOLS), 0.1, 0.6, ((1, 4), (2, 4)), jnp.float32)
    crack_mask = set_ends((jax.random.randint(splits[3], (NROWS, NCOLS // 128), 0, 4) < 3).astype(jnp.int32), jax.random.fold_in(splits[3], 1), 0, 1)
    node_panel = noise(splits[4], (NR, NC, 3, P_SIZE), 0.07, 0.41992188, ((0, 4), (1, 4), (3, 32)))
    return dict(coefficients=coefficients, noise_sigma=noise_sigma, residual=residual, crack_mask=crack_mask, node_panel=node_panel)


def corner_shapes(rows, cols):
    vertical = ((jnp.arange(rows) % EL).astype(jnp.float32) + 0.5) / EL
    horizontal = ((jnp.arange(cols) % EL).astype(jnp.float32) + 0.5) / EL
    lower = vertical[:, None]
    right = horizontal[None, :]
    return jnp.stack([(1.0 - lower) * (1.0 - right), (1.0 - lower) * right, lower * (1.0 - right), lower * right])


def reference(coefficients, noise_sigma, residual, crack_mask, node_panel):
    extended = jnp.pad(node_panel, ((0, 1), (0, 1), (0, 0), (0, 0)))
    shapes = corner_shapes(EL, NCOLS)

    def strip(totals, index):
        hess_sum, grad_sum = totals
        first = (index * EL).astype(jnp.int32)
        coef_rows = lax.dynamic_slice_in_dim(coefficients, first, EL, 2).astype(jnp.float32)
        sigma_rows = lax.dynamic_slice_in_dim(noise_sigma, first, EL, 1)
        resid_rows = lax.dynamic_slice_in_dim(residual, first, EL, 1)
        mask_rows = lax.dynamic_slice_in_dim(crack_mask, first, EL, 0)
        live_rows = jnp.repeat(mask_rows.astype(jnp.float32), 128, axis=1)
        pixel_scale = live_rows[None] / sigma_rows
        design = ((shapes[:, None, None] * pixel_scale[None, None]) * coef_rows[None]).astype(jnp.bfloat16)
        design = design.reshape(4, 3, CAMS, EL, NC, EL).transpose(0, 1, 4, 2, 3, 5).reshape(12, NC, CAMS * EL * EL)
        nodes = lax.dynamic_slice_in_dim(extended, index.astype(jnp.int32), 2, 0)
        corners = jnp.stack([nodes[0, :-1], nodes[0, 1:], nodes[1, :-1], nodes[1, 1:]], axis=1)
        corners = corners.reshape(NC, 12, P_SIZE)
        sensitivity = jnp.einsum("kep,ekq->epq", design.astype(jnp.float32), corners.astype(jnp.float32),
                                 precision=lax.Precision.HIGHEST).astype(jnp.bfloat16)
        flat = sensitivity.reshape(NC * CAMS * EL * EL, P_SIZE)
        weighted = (pixel_scale * resid_rows).astype(jnp.bfloat16)
        weighted = weighted.reshape(CAMS, EL, NC, EL).transpose(2, 0, 1, 3).reshape(NC * CAMS * EL * EL)
        hess_sum = hess_sum + jnp.dot(flat.T, flat, preferred_element_type=jnp.float32)
        grad_sum = grad_sum + jnp.dot(weighted, flat, preferred_element_type=jnp.float32)
        return (hess_sum, grad_sum), None

    start = (jnp.zeros((P_SIZE, P_SIZE), jnp.float32), jnp.zeros((P_SIZE,), jnp.float32))
    (hessian, gradient), _ = lax.scan(strip, start, jnp.arange(NR, dtype=jnp.int32))
    return hessian, gradient
```

```python
import jax
import jax.numpy as jnp
from jax import lax
from jax.sharding import PartitionSpec as P

EL = 8
CAMS = 2
LANES = 128
HIGHEST = lax.Precision.HIGHEST

PARAM_ORDER = (8, 4, 2, 1, 16)
TILE_ORDER = (8, 2, 4, 1)


def corner_shapes(rows, cols):
    vertical = ((jnp.arange(rows) % EL).astype(jnp.float32) + 0.5) / EL
    horizontal = ((jnp.arange(cols) % EL).astype(jnp.float32) + 0.5) / EL
    lower = vertical[:, None]
    right = horizontal[None, :]
    return jnp.stack(
        [(1.0 - lower) * (1.0 - right), (1.0 - lower) * right, lower * (1.0 - right), lower * right]
    )


def doubling_gather(piece, axes, order):
    size = 1
    for bit in order:
        size *= 2
    me = lax.axis_index(axes)
    data = piece[None]
    for bit in order:
        theirs = lax.ppermute(data, axes, [(i, i ^ bit) for i in range(size)])
        data = jnp.concatenate([data, theirs], axis=0)
    wanted = me ^ jnp.arange(size, dtype=jnp.int32)
    position = jnp.zeros((size,), jnp.int32)
    for step, bit in enumerate(order):
        position = position | (((wanted // bit) % 2) << step)
    return jnp.take(data, position, axis=0)


def as_lanes(flat, dtype):
    rows = -(-flat.shape[0] // (8 * LANES)) * 8
    flat = jnp.pad(flat.astype(dtype), (0, rows * LANES - flat.shape[0]))
    return flat.reshape(rows, LANES)


def element_corners(nodes):
    extended = jnp.pad(nodes, ((0, 1), (0, 1), (0, 0), (0, 0)))
    corners = jnp.stack(
        [extended[:-1, :-1], extended[:-1, 1:], extended[1:, :-1], extended[1:, 1:]], axis=2
    )
    return corners.reshape(nodes.shape[0] * nodes.shape[1], 12, nodes.shape[3])


def on_device(coefficients, noise_sigma, residual, crack_mask, node_panel):
    n_param = lax.axis_size("param")
    n_row = lax.axis_size("row")
    n_col = lax.axis_size("col")
    tiles = n_row * n_col
    per_block = n_param // tiles
    rows = noise_sigma.shape[1]
    cols = noise_sigma.shape[2]
    elem_rows = rows // EL
    elem_cols = cols // EL
    node_rows, node_cols, comps, width = node_panel.shape
    elements = elem_rows * elem_cols

    shapes = corner_shapes(rows, cols)
    live_rows = jnp.repeat(crack_mask.astype(jnp.float32), 128, axis=1)
    pixel_scale = live_rows[None] / noise_sigma
    design = (
        shapes[:, None, None] * pixel_scale[None, None] * coefficients.astype(jnp.float32)[None]
    ).astype(jnp.bfloat16)
    design = design.reshape(4, 3, CAMS, elem_rows, EL, elem_cols, EL).transpose(3, 5, 0, 1, 2, 4, 6)
    design = design.reshape(elements, 12, CAMS * EL * EL)
    weighted = (pixel_scale * residual).astype(jnp.bfloat16)
    weighted = weighted.reshape(CAMS, elem_rows, EL, elem_cols, EL).transpose(1, 3, 0, 2, 4)
    weighted = weighted.reshape(elements, CAMS * EL * EL)
    gram = jnp.einsum("eip,ejp->eij", design, design, preferred_element_type=jnp.float32)
    proj = jnp.einsum("eip,ep->ei", design, weighted, preferred_element_type=jnp.float32)

    payload = jnp.concatenate([node_panel.reshape(-1).astype(jnp.float32), gram.reshape(-1), proj.reshape(-1)])
    own = doubling_gather(as_lanes(payload, jnp.float32), ("row", "col"), TILE_ORDER)
    own = own.reshape(tiles, -1)
    n_nodes = node_rows * node_cols * comps * width
    n_gram = elements * 144
    own_nodes = own[:, :n_nodes].reshape(n_row, n_col, node_rows, node_cols, comps, width)
    own_nodes = own_nodes.transpose(0, 2, 1, 3, 4, 5).reshape(n_row * node_rows, n_col * node_cols, comps, width)
    grams = own[:, n_nodes : n_nodes + n_gram].reshape(n_row, n_col, elem_rows, elem_cols, 12, 12)
    grams = grams.transpose(0, 2, 1, 3, 4, 5).reshape(-1, 12, 12)
    projs = own[:, n_nodes + n_gram : n_nodes + n_gram + elements * 12]
    projs = projs.reshape(n_row, n_col, elem_rows, elem_cols, 12).transpose(0, 2, 1, 3, 4).reshape(-1, 12)

    route = []
    for b in range(n_param):
        for t in range(tiles):
            route.append((b * tiles + t, (per_block * t + b % per_block) * tiles + b // per_block))
    moved = lax.ppermute(as_lanes(node_panel.reshape(-1), jnp.bfloat16), ("param", "row", "col"), route)
    cross = doubling_gather(moved, "param", PARAM_ORDER).reshape(n_param, -1)[:, : node_rows * node_cols * comps * width]
    cross = cross.reshape(n_row, n_col, per_block, node_rows, node_cols, comps, width)
    cross = cross.transpose(0, 3, 1, 4, 5, 2, 6)
    cross = cross.reshape(n_row * node_rows, n_col * node_cols, comps, per_block * width)

    rows_of = element_corners(own_nodes.astype(jnp.bfloat16)).astype(jnp.float32)
    cols_of = element_corners(cross).astype(jnp.float32)
    weighted_cols = grams[:, :, 0, None] * cols_of[:, None, 0, :]
    for j in range(1, 12):
        weighted_cols = weighted_cols + grams[:, :, j, None] * cols_of[:, None, j, :]
    hessian = jnp.einsum("eip,eiq->pq", rows_of, weighted_cols, precision=HIGHEST)
    gradient = jnp.einsum("eip,ei->p", rows_of, projs, precision=HIGHEST)
    share = width // tiles
    gradient = lax.dynamic_slice(gradient, (lax.axis_index(("row", "col")) * share,), (share,))
    return (hessian, gradient)


def solution(mesh):
    in_specs = (
        P(None, None, "row", "col"),
        P(None, "row", "col"),
        P(None, "row", "col"),
        P("row", "col"),
        P("row", "col", None, "param"),
    )
    out_specs = (P("param", ("row", "col")), P(("param", "row", "col")))
    return jax.shard_map(
        on_device, mesh=mesh, in_specs=in_specs, out_specs=out_specs, check_vma=False
    )
```

```python
import jax
import jax.numpy as jnp
from jax import lax
from jax.sharding import PartitionSpec as P

EL = 8
CAMS = 2
LANES = 128
HIGHEST = lax.Precision.HIGHEST

PARAM_ORDER = (8, 4, 2, 1, 16)
TILE_ORDER = (8, 2, 4, 1)


def corner_shapes(rows, cols):
    vertical = ((jnp.arange(rows) % EL).astype(jnp.float32) + 0.5) / EL
    horizontal = ((jnp.arange(cols) % EL).astype(jnp.float32) + 0.5) / EL
    lower = vertical[:, None]
    right = horizontal[None, :]
    return jnp.stack(
        [(1.0 - lower) * (1.0 - right), (1.0 - lower) * right, lower * (1.0 - right), lower * right]
    )


def doubling_gather(piece, axes, order):
    size = 1
    for bit in order:
        size *= 2
    me = lax.axis_index(axes)
    data = piece[None]
    for bit in order:
        theirs = lax.ppermute(data, axes, [(i, i ^ bit) for i in range(size)])
        data = jnp.concatenate([data, theirs], axis=0)
    wanted = me ^ jnp.arange(size, dtype=jnp.int32)
    position = jnp.zeros((size,), jnp.int32)
    for step, bit in enumerate(order):
        position = position | (((wanted // bit) % 2) << step)
    return jnp.take(data, position, axis=0)


def as_lanes(flat, dtype):
    rows = -(-flat.shape[0] // (8 * LANES)) * 8
    flat = jnp.pad(flat.astype(dtype), (0, rows * LANES - flat.shape[0]))
    return flat.reshape(rows, LANES)


def element_corners(nodes):
    extended = jnp.pad(nodes, ((0, 1), (0, 1), (0, 0), (0, 0)))
    corners = jnp.stack(
        [extended[:-1, :-1], extended[:-1, 1:], extended[1:, :-1], extended[1:, 1:]], axis=0
    )
    corners = corners.transpose(0, 3, 1, 2, 4)
    return corners.reshape(12, nodes.shape[0] * nodes.shape[1], nodes.shape[3])


def on_device(coefficients, noise_sigma, residual, crack_mask, node_panel):
    n_param = lax.axis_size("param")
    n_row = lax.axis_size("row")
    n_col = lax.axis_size("col")
    tiles = n_row * n_col
    per_block = n_param // tiles
    rows = noise_sigma.shape[1]
    cols = noise_sigma.shape[2]
    elem_rows = rows // EL
    elem_cols = cols // EL
    node_rows, node_cols, comps, width = node_panel.shape
    elements = elem_rows * elem_cols

    shapes = corner_shapes(rows, cols)
    live_rows = jnp.repeat(crack_mask.astype(jnp.float32), 128, axis=1)
    pixel_scale = live_rows[None] / noise_sigma
    design = (
        shapes[:, None, None] * pixel_scale[None, None] * coefficients.astype(jnp.float32)[None]
    ).astype(jnp.bfloat16)
    design = design.reshape(4, 3, CAMS, elem_rows, EL, elem_cols, EL).transpose(3, 5, 0, 1, 2, 4, 6)
    design = design.reshape(elements, 12, CAMS * EL * EL)
    weighted = (pixel_scale * residual).astype(jnp.bfloat16)
    weighted = weighted.reshape(CAMS, elem_rows, EL, elem_cols, EL).transpose(1, 3, 0, 2, 4)
    weighted = weighted.reshape(elements, CAMS * EL * EL)
    gram = jnp.einsum("eip,ejp->eij", design, design, preferred_element_type=jnp.float32)
    proj = jnp.einsum("eip,ep->ei", design, weighted, preferred_element_type=jnp.float32)

    payload = jnp.concatenate([node_panel.reshape(-1).astype(jnp.float32), gram.reshape(-1), proj.reshape(-1)])
    own = doubling_gather(as_lanes(payload, jnp.float32), ("row", "col"), TILE_ORDER)
    own = own.reshape(tiles, -1)
    n_nodes = node_rows * node_cols * comps * width
    n_gram = elements * 144
    own_nodes = own[:, :n_nodes].reshape(n_row, n_col, node_rows, node_cols, comps, width)
    own_nodes = own_nodes.transpose(0, 2, 1, 3, 4, 5).reshape(n_row * node_rows, n_col * node_cols, comps, width)
    grams = own[:, n_nodes : n_nodes + n_gram].reshape(n_row, n_col, elem_rows, elem_cols, 12, 12)
    grams = grams.transpose(0, 2, 1, 3, 4, 5).reshape(-1, 12, 12)
    projs = own[:, n_nodes + n_gram : n_nodes + n_gram + elements * 12]
    projs = projs.reshape(n_row, n_col, elem_rows, elem_cols, 12).transpose(0, 2, 1, 3, 4).reshape(-1, 12)

    route = []
    for b in range(n_param):
        for t in range(tiles):
            route.append((b * tiles + t, (per_block * t + b % per_block) * tiles + b // per_block))
    moved = lax.ppermute(as_lanes(node_panel.reshape(-1), jnp.bfloat16), ("param", "row", "col"), route)
    cross = doubling_gather(moved, "param", PARAM_ORDER).reshape(n_param, -1)[:, : node_rows * node_cols * comps * width]
    cross = cross.reshape(n_row, n_col, per_block, node_rows, node_cols, comps, width)
    cross = cross.transpose(0, 3, 1, 4, 5, 2, 6)
    cross = cross.reshape(n_row * node_rows, n_col * node_cols, comps, per_block * width)

    rows_of = element_corners(own_nodes.astype(jnp.bfloat16))
    cols_of = element_corners(cross).astype(jnp.float32)
    weighted_cols = jnp.sum(grams.transpose(1, 2, 0)[:, :, :, None] * cols_of[None], axis=1)
    high = weighted_cols.astype(jnp.bfloat16)
    low = (weighted_cols - high.astype(jnp.float32)).astype(jnp.bfloat16)
    proj_t = projs.T[:, :, None]
    proj_high = proj_t.astype(jnp.bfloat16)
    proj_low = (proj_t - proj_high.astype(jnp.float32)).astype(jnp.bfloat16)
    operand = jnp.concatenate([high, low, proj_high, proj_low], axis=2)
    product = jnp.einsum("iep,ieq->pq", rows_of, operand, preferred_element_type=jnp.float32)
    cols = cross.shape[3]
    hessian = product[:, :cols] + product[:, cols : 2 * cols]
    gradient = product[:, 2 * cols] + product[:, 2 * cols + 1]
    share = width // tiles
    gradient = lax.dynamic_slice(gradient, (lax.axis_index(("row", "col")) * share,), (share,))
    return (hessian, gradient)


def solution(mesh):
    in_specs = (
        P(None, None, "row", "col"),
        P(None, "row", "col"),
        P(None, "row", "col"),
        P("row", "col"),
        P("row", "col", None, "param"),
    )
    out_specs = (P("param", ("row", "col")), P(("param", "row", "col")))
    return jax.shard_map(
        on_device, mesh=mesh, in_specs=in_specs, out_specs=out_specs, check_vma=False
    )
```

```python
import jax
import jax.numpy as jnp
from jax import lax
from jax.sharding import PartitionSpec as P

EL = 8
CAMS = 2
LANES = 128
HIGHEST = lax.Precision.HIGHEST

PARAM_ORDER = (8, 4, 2, 1, 16)
TILE_ORDER = (8, 2, 4, 1)


def corner_shapes(rows, cols):
    vertical = ((jnp.arange(rows) % EL).astype(jnp.float32) + 0.5) / EL
    horizontal = ((jnp.arange(cols) % EL).astype(jnp.float32) + 0.5) / EL
    lower = vertical[:, None]
    right = horizontal[None, :]
    return jnp.stack(
        [(1.0 - lower) * (1.0 - right), (1.0 - lower) * right, lower * (1.0 - right), lower * right]
    )


def doubling_gather(piece, axes, order):
    size = 1
    for bit in order:
        size *= 2
    me = lax.axis_index(axes)
    data = piece[None]
    for bit in order:
        theirs = lax.ppermute(data, axes, [(i, i ^ bit) for i in range(size)])
        data = jnp.concatenate([data, theirs], axis=0)
    wanted = me ^ jnp.arange(size, dtype=jnp.int32)
    position = jnp.zeros((size,), jnp.int32)
    for step, bit in enumerate(order):
        position = position | (((wanted // bit) % 2) << step)
    return jnp.take(data, position, axis=0)


def as_lanes(flat, dtype):
    rows = -(-flat.shape[0] // (8 * LANES)) * 8
    flat = jnp.pad(flat.astype(dtype), (0, rows * LANES - flat.shape[0]))
    return flat.reshape(rows, LANES)


def element_corners(nodes):
    extended = jnp.pad(nodes, ((0, 1), (0, 1), (0, 0), (0, 0)))
    corners = jnp.stack(
        [extended[:-1, :-1], extended[:-1, 1:], extended[1:, :-1], extended[1:, 1:]], axis=0
    )
    corners = corners.transpose(0, 3, 1, 2, 4)
    return corners.reshape(12, nodes.shape[0] * nodes.shape[1], nodes.shape[3])


def on_device(coefficients, noise_sigma, residual, crack_mask, node_panel):
    n_param = lax.axis_size("param")
    n_row = lax.axis_size("row")
    n_col = lax.axis_size("col")
    tiles = n_row * n_col
    per_block = n_param // tiles
    rows = noise_sigma.shape[1]
    cols = noise_sigma.shape[2]
    elem_rows = rows // EL
    elem_cols = cols // EL
    node_rows, node_cols, comps, width = node_panel.shape
    elements = elem_rows * elem_cols

    shapes = corner_shapes(rows, cols)
    live_rows = jnp.repeat(crack_mask.astype(jnp.float32), 128, axis=1)
    pixel_scale = live_rows[None] / noise_sigma
    design = (
        shapes[:, None, None] * pixel_scale[None, None] * coefficients.astype(jnp.float32)[None]
    ).astype(jnp.bfloat16)
    design = design.reshape(4, 3, CAMS, elem_rows, EL, elem_cols, EL).transpose(3, 5, 0, 1, 2, 4, 6)
    design = design.reshape(elements, 12, CAMS * EL * EL)
    weighted = (pixel_scale * residual).astype(jnp.bfloat16)
    weighted = weighted.reshape(CAMS, elem_rows, EL, elem_cols, EL).transpose(1, 3, 0, 2, 4)
    weighted = weighted.reshape(elements, CAMS * EL * EL)
    gram = jnp.einsum("eip,ejp->eij", design, design, preferred_element_type=jnp.float32)
    proj = jnp.einsum("eip,ep->ei", design, weighted, preferred_element_type=jnp.float32)

    payload = jnp.concatenate([node_panel.reshape(-1).astype(jnp.float32), gram.reshape(-1), proj.reshape(-1)])
    piece = as_lanes(payload, jnp.float32)
    slots = jnp.zeros((tiles,) + piece.shape, jnp.float32)
    slots = lax.dynamic_update_slice(slots, piece[None], (lax.axis_index(("row", "col")), 0, 0))
    own = lax.psum(slots, ("row", "col"))
    own = own.reshape(tiles, -1)
    n_nodes = node_rows * node_cols * comps * width
    n_gram = elements * 144
    own_nodes = own[:, :n_nodes].reshape(n_row, n_col, node_rows, node_cols, comps, width)
    own_nodes = own_nodes.transpose(0, 2, 1, 3, 4, 5).reshape(n_row * node_rows, n_col * node_cols, comps, width)
    grams = own[:, n_nodes : n_nodes + n_gram].reshape(n_row, n_col, elem_rows, elem_cols, 12, 12)
    grams = grams.transpose(0, 2, 1, 3, 4, 5).reshape(-1, 12, 12)
    projs = own[:, n_nodes + n_gram : n_nodes + n_gram + elements * 12]
    projs = projs.reshape(n_row, n_col, elem_rows, elem_cols, 12).transpose(0, 2, 1, 3, 4).reshape(-1, 12)

    route = []
    for b in range(n_param):
        for t in range(tiles):
            route.append((b * tiles + t, (per_block * t + b % per_block) * tiles + b // per_block))
    moved = lax.ppermute(as_lanes(node_panel.reshape(-1), jnp.bfloat16), ("param", "row", "col"), route)
    cross = doubling_gather(moved, "param", PARAM_ORDER).reshape(n_param, -1)[:, : node_rows * node_cols * comps * width]
    cross = cross.reshape(n_row, n_col, per_block, node_rows, node_cols, comps, width)
    cross = cross.transpose(0, 3, 1, 4, 5, 2, 6)
    cross = cross.reshape(n_row * node_rows, n_col * node_cols, comps, per_block * width)

    rows_of = element_corners(own_nodes.astype(jnp.bfloat16))
    cols_of = element_corners(cross)
    weighted_rows = jnp.sum(grams.transpose(1, 2, 0)[:, :, :, None] * rows_of.astype(jnp.float32)[:, None], axis=0)
    high = lax.reduce_precision(weighted_rows, exponent_bits=8, mantissa_bits=7)
    low = weighted_rows - high
    stacked = jnp.concatenate([high.astype(jnp.bfloat16), low.astype(jnp.bfloat16)], axis=2)
    product = jnp.einsum("jep,jeq->pq", stacked, cols_of, preferred_element_type=jnp.float32)
    hessian = product[:width] + product[width:]
    gradient = jnp.einsum("iep,ie->p", rows_of.astype(jnp.float32), projs.T, precision=HIGHEST)
    share = width // tiles
    gradient = lax.dynamic_slice(gradient, (lax.axis_index(("row", "col")) * share,), (share,))
    return (hessian, gradient)


def solution(mesh):
    in_specs = (
        P(None, None, "row", "col"),
        P(None, "row", "col"),
        P(None, "row", "col"),
        P("row", "col"),
        P("row", "col", None, "param"),
    )
    out_specs = (P("param", ("row", "col")), P(("param", "row", "col")))
    return jax.shard_map(
        on_device, mesh=mesh, in_specs=in_specs, out_specs=out_specs, check_vma=False
    )
```

```python
import jax
import jax.numpy as jnp
from jax import lax
from jax.sharding import PartitionSpec as P

EL = 8
CAMS = 2
LANES = 128
HIGHEST = lax.Precision.HIGHEST

PARAM_ORDER = (8, 4, 2, 1, 16)
TILE_ORDER = (8, 2, 4, 1)


def corner_shapes(rows, cols):
    vertical = ((jnp.arange(rows) % EL).astype(jnp.float32) + 0.5) / EL
    horizontal = ((jnp.arange(cols) % EL).astype(jnp.float32) + 0.5) / EL
    lower = vertical[:, None]
    right = horizontal[None, :]
    return jnp.stack(
        [(1.0 - lower) * (1.0 - right), (1.0 - lower) * right, lower * (1.0 - right), lower * right]
    )


def doubling_gather(piece, axes, order):
    size = 1
    for bit in order:
        size *= 2
    me = lax.axis_index(axes)
    data = piece[None]
    for bit in order:
        theirs = lax.ppermute(data, axes, [(i, i ^ bit) for i in range(size)])
        data = jnp.concatenate([data, theirs], axis=0)
    wanted = me ^ jnp.arange(size, dtype=jnp.int32)
    position = jnp.zeros((size,), jnp.int32)
    for step, bit in enumerate(order):
        position = position | (((wanted // bit) % 2) << step)
    return jnp.take(data, position, axis=0)


def as_lanes(flat, dtype):
    rows = -(-flat.shape[0] // (8 * LANES)) * 8
    flat = jnp.pad(flat.astype(dtype), (0, rows * LANES - flat.shape[0]))
    return flat.reshape(rows, LANES)


def element_corners(nodes):
    extended = jnp.pad(nodes, ((0, 1), (0, 1), (0, 0), (0, 0)))
    corners = jnp.stack(
        [extended[:-1, :-1], extended[:-1, 1:], extended[1:, :-1], extended[1:, 1:]], axis=0
    )
    corners = corners.transpose(0, 3, 1, 2, 4)
    return corners.reshape(12, nodes.shape[0] * nodes.shape[1], nodes.shape[3])


def on_device(coefficients, noise_sigma, residual, crack_mask, node_panel):
    n_param = lax.axis_size("param")
    n_row = lax.axis_size("row")
    n_col = lax.axis_size("col")
    tiles = n_row * n_col
    per_block = n_param // tiles
    rows = noise_sigma.shape[1]
    cols = noise_sigma.shape[2]
    elem_rows = rows // EL
    elem_cols = cols // EL
    node_rows, node_cols, comps, width = node_panel.shape
    elements = elem_rows * elem_cols

    shapes = corner_shapes(rows, cols)
    live_rows = jnp.repeat(crack_mask.astype(jnp.float32), 128, axis=1)
    pixel_scale = live_rows[None] / noise_sigma
    design = (
        shapes[:, None, None] * pixel_scale[None, None] * coefficients.astype(jnp.float32)[None]
    ).astype(jnp.bfloat16)
    design = design.reshape(4, 3, CAMS, elem_rows, EL, elem_cols, EL).transpose(3, 5, 0, 1, 2, 4, 6)
    design = design.reshape(elements, 12, CAMS * EL * EL)
    weighted = (pixel_scale * residual).astype(jnp.bfloat16)
    weighted = weighted.reshape(CAMS, elem_rows, EL, elem_cols, EL).transpose(1, 3, 0, 2, 4)
    weighted = weighted.reshape(elements, CAMS * EL * EL)
    gram = jnp.einsum("eip,ejp->eij", design, design, preferred_element_type=jnp.float32)
    proj = jnp.einsum("eip,ep->ei", design, weighted, preferred_element_type=jnp.float32)

    payload = jnp.concatenate([node_panel.reshape(-1).astype(jnp.float32), gram.reshape(-1), proj.reshape(-1)])
    own = doubling_gather(as_lanes(payload, jnp.float32), ("row", "col"), TILE_ORDER)
    own = own.reshape(tiles, -1)
    n_nodes = node_rows * node_cols * comps * width
    n_gram = elements * 144
    own_nodes = own[:, :n_nodes].reshape(n_row, n_col, node_rows, node_cols, comps, width)
    own_nodes = own_nodes.transpose(0, 2, 1, 3, 4, 5).reshape(n_row * node_rows, n_col * node_cols, comps, width)
    grams = own[:, n_nodes : n_nodes + n_gram].reshape(n_row, n_col, elem_rows, elem_cols, 12, 12)
    grams = grams.transpose(0, 2, 1, 3, 4, 5).reshape(-1, 12, 12)
    projs = own[:, n_nodes + n_gram : n_nodes + n_gram + elements * 12]
    projs = projs.reshape(n_row, n_col, elem_rows, elem_cols, 12).transpose(0, 2, 1, 3, 4).reshape(-1, 12)

    route = []
    for b in range(n_param):
        for t in range(tiles):
            route.append((b * tiles + t, (per_block * t + b % per_block) * tiles + b // per_block))
    moved = lax.ppermute(as_lanes(node_panel.reshape(-1), jnp.bfloat16), ("param", "row", "col"), route)
    cross = doubling_gather(moved, "param", PARAM_ORDER).reshape(n_param, -1)[:, : node_rows * node_cols * comps * width]
    cross = cross.reshape(n_row, n_col, per_block, node_rows, node_cols, comps, width)
    cross = cross.transpose(0, 3, 1, 4, 5, 2, 6)
    cross = cross.reshape(n_row * node_rows, n_col * node_cols, comps, per_block * width)

    rows_of = element_corners(own_nodes.astype(jnp.bfloat16))
    cols_of = element_corners(cross)
    weighted_rows = jnp.sum(grams.transpose(1, 2, 0)[:, :, :, None] * rows_of.astype(jnp.float32)[:, None], axis=0)
    high = lax.reduce_precision(weighted_rows, exponent_bits=8, mantissa_bits=7)
    low = weighted_rows - high
    stacked = jnp.concatenate([high.astype(jnp.bfloat16), low.astype(jnp.bfloat16)], axis=2)
    product = jnp.einsum("jep,jeq->pq", stacked, cols_of, preferred_element_type=jnp.float32)
    hessian = product[:width] + product[width:]
    gradient = jnp.einsum("iep,ie->p", rows_of.astype(jnp.float32), projs.T, precision=HIGHEST)
    share = width // tiles
    gradient = lax.dynamic_slice(gradient, (lax.axis_index(("row", "col")) * share,), (share,))
    return (hessian, gradient)


def solution(mesh):
    in_specs = (
        P(None, None, "row", "col"),
        P(None, "row", "col"),
        P(None, "row", "col"),
        P("row", "col"),
        P("row", "col", None, "param"),
    )
    out_specs = (P("param", ("row", "col")), P(("param", "row", "col")))
    return jax.shard_map(
        on_device, mesh=mesh, in_specs=in_specs, out_specs=out_specs, check_vma=False
    )
```

```python
import jax
import jax.numpy as jnp
from jax import lax
from jax.sharding import PartitionSpec as P

EL = 8
CAMS = 2
LANES = 128
HIGHEST = lax.Precision.HIGHEST

PARAM_ORDER = (8, 4, 2, 1, 16)


def corner_shapes(rows, cols):
    vertical = ((jnp.arange(rows) % EL).astype(jnp.float32) + 0.5) / EL
    horizontal = ((jnp.arange(cols) % EL).astype(jnp.float32) + 0.5) / EL
    lower = vertical[:, None]
    right = horizontal[None, :]
    return jnp.stack(
        [(1.0 - lower) * (1.0 - right), (1.0 - lower) * right, lower * (1.0 - right), lower * right]
    )


def doubling_gather(piece, axes, order):
    size = 1
    for bit in order:
        size *= 2
    me = lax.axis_index(axes)
    data = piece[None]
    for bit in order:
        theirs = lax.ppermute(data, axes, [(i, i ^ bit) for i in range(size)])
        data = jnp.concatenate([data, theirs], axis=0)
    wanted = me ^ jnp.arange(size, dtype=jnp.int32)
    position = jnp.zeros((size,), jnp.int32)
    for step, bit in enumerate(order):
        position = position | (((wanted // bit) % 2) << step)
    return jnp.take(data, position, axis=0)


def as_lanes(flat, dtype):
    rows = -(-flat.shape[0] // (8 * LANES)) * 8
    flat = jnp.pad(flat.astype(dtype), (0, rows * LANES - flat.shape[0]))
    return flat.reshape(rows, LANES)


def element_corners(nodes):
    extended = jnp.pad(nodes, ((0, 1), (0, 1), (0, 0), (0, 0)))
    corners = jnp.stack(
        [extended[:-1, :-1], extended[:-1, 1:], extended[1:, :-1], extended[1:, 1:]], axis=0
    )
    corners = corners.transpose(0, 3, 1, 2, 4)
    return corners.reshape(12, nodes.shape[0] * nodes.shape[1], nodes.shape[3])


def on_device(coefficients, noise_sigma, residual, crack_mask, node_panel):
    n_param = lax.axis_size("param")
    n_row = lax.axis_size("row")
    n_col = lax.axis_size("col")
    tiles = n_row * n_col
    per_block = n_param // tiles
    rows = noise_sigma.shape[1]
    cols = noise_sigma.shape[2]
    elem_rows = rows // EL
    elem_cols = cols // EL
    node_rows, node_cols, comps, width = node_panel.shape
    elements = elem_rows * elem_cols

    shapes = corner_shapes(rows, cols)
    live_rows = jnp.repeat(crack_mask.astype(jnp.float32), 128, axis=1)
    pixel_scale = live_rows[None] / noise_sigma
    design = (
        shapes[:, None, None] * pixel_scale[None, None] * coefficients.astype(jnp.float32)[None]
    ).astype(jnp.bfloat16)
    design = design.reshape(4, 3, CAMS, elem_rows, EL, elem_cols, EL).transpose(3, 5, 0, 1, 2, 4, 6)
    design = design.reshape(elements, 12, CAMS * EL * EL)
    weighted = (pixel_scale * residual).astype(jnp.bfloat16)
    weighted = weighted.reshape(CAMS, elem_rows, EL, elem_cols, EL).transpose(1, 3, 0, 2, 4)
    weighted = weighted.reshape(elements, CAMS * EL * EL)
    gram = jnp.einsum("eip,ejp->eij", design, design, preferred_element_type=jnp.float32)
    proj = jnp.einsum("eip,ep->ei", design, weighted, preferred_element_type=jnp.float32)

    n_nodes = node_rows * node_cols * comps * width
    n_gram = elements * 144
    payload = jnp.concatenate([node_panel.reshape(-1).astype(jnp.float32), gram.reshape(-1), proj.reshape(-1)])
    route = []
    for b in range(n_param):
        for t in range(tiles):
            route.append((b * tiles + t, (per_block * t + b % per_block) * tiles + b // per_block))
    moved = lax.ppermute(as_lanes(payload, jnp.float32), ("param", "row", "col"), route)
    gathered = doubling_gather(moved, "param", PARAM_ORDER).reshape(tiles, per_block, -1)
    cross = gathered[:, :, :n_nodes].astype(jnp.bfloat16)
    cross = cross.reshape(n_row, n_col, per_block, node_rows, node_cols, comps, width)
    cross = cross.transpose(0, 3, 1, 4, 5, 2, 6)
    cross = cross.reshape(n_row * node_rows, n_col * node_cols, comps, per_block * width)
    grams = gathered[:, 0, n_nodes : n_nodes + n_gram].reshape(n_row, n_col, elem_rows, elem_cols, 12, 12)
    grams = grams.transpose(0, 2, 1, 3, 4, 5).reshape(-1, 12, 12)
    projs = gathered[:, 0, n_nodes + n_gram : n_nodes + n_gram + elements * 12]
    projs = projs.reshape(n_row, n_col, elem_rows, elem_cols, 12).transpose(0, 2, 1, 3, 4).reshape(-1, 12)

    half = lax.axis_index("param") % per_block
    mine = lax.dynamic_index_in_dim(gathered[:, :, :n_nodes], half, axis=1, keepdims=False)
    back = []
    for x in range(n_param):
        for t in range(tiles):
            back.append((x * tiles + t, (per_block * t + x % per_block) * tiles + x // per_block))
    own = lax.ppermute(as_lanes(mine.reshape(-1), jnp.bfloat16), ("param", "row", "col"), back)
    own_nodes = own.reshape(-1)[: tiles * n_nodes].reshape(n_row, n_col, node_rows, node_cols, comps, width)
    own_nodes = own_nodes.transpose(0, 2, 1, 3, 4, 5).reshape(n_row * node_rows, n_col * node_cols, comps, width)

    rows_of = element_corners(own_nodes)
    cols_of = element_corners(cross)
    weighted_rows = jnp.sum(grams.transpose(1, 2, 0)[:, :, :, None] * rows_of.astype(jnp.float32)[:, None], axis=0)
    high = lax.reduce_precision(weighted_rows, exponent_bits=8, mantissa_bits=7)
    low = weighted_rows - high
    stacked = jnp.concatenate([high.astype(jnp.bfloat16), low.astype(jnp.bfloat16)], axis=2)
    product = jnp.einsum("jep,jeq->pq", stacked, cols_of, preferred_element_type=jnp.float32)
    hessian = product[:width] + product[width:]
    gradient = jnp.einsum("iep,ie->p", rows_of.astype(jnp.float32), projs.T, precision=HIGHEST)
    share = width // tiles
    gradient = lax.dynamic_slice(gradient, (lax.axis_index(("row", "col")) * share,), (share,))
    return (hessian, gradient)


def solution(mesh):
    in_specs = (
        P(None, None, "row", "col"),
        P(None, "row", "col"),
        P(None, "row", "col"),
        P("row", "col"),
        P("row", "col", None, "param"),
    )
    out_specs = (P("param", ("row", "col")), P(("param", "row", "col")))
    return jax.shard_map(
        on_device, mesh=mesh, in_specs=in_specs, out_specs=out_specs, check_vma=False
    )
```

```python
import jax
import jax.numpy as jnp
from jax import lax
from jax.sharding import PartitionSpec as P

EL = 8
CAMS = 2
LANES = 128
HIGHEST = lax.Precision.HIGHEST

def corner_shapes(rows, cols):
    vertical = ((jnp.arange(rows) % EL).astype(jnp.float32) + 0.5) / EL
    horizontal = ((jnp.arange(cols) % EL).astype(jnp.float32) + 0.5) / EL
    lower = vertical[:, None]
    right = horizontal[None, :]
    return jnp.stack(
        [(1.0 - lower) * (1.0 - right), (1.0 - lower) * right, lower * (1.0 - right), lower * right]
    )


def exchange_gather(piece, axes):
    size = lax.axis_size(axes)
    copies = jnp.broadcast_to(piece[None], (size,) + piece.shape)
    return lax.all_to_all(copies, axes, 0, 0, tiled=False)


def as_lanes(flat, dtype):
    rows = -(-flat.shape[0] // (8 * LANES)) * 8
    flat = jnp.pad(flat.astype(dtype), (0, rows * LANES - flat.shape[0]))
    return flat.reshape(rows, LANES)


def element_corners(nodes):
    extended = jnp.pad(nodes, ((0, 1), (0, 1), (0, 0), (0, 0)))
    corners = jnp.stack(
        [extended[:-1, :-1], extended[:-1, 1:], extended[1:, :-1], extended[1:, 1:]], axis=0
    )
    corners = corners.transpose(0, 3, 1, 2, 4)
    return corners.reshape(12, nodes.shape[0] * nodes.shape[1], nodes.shape[3])


def on_device(coefficients, noise_sigma, residual, crack_mask, node_panel):
    n_param = lax.axis_size("param")
    n_row = lax.axis_size("row")
    n_col = lax.axis_size("col")
    tiles = n_row * n_col
    per_block = n_param // tiles
    rows = noise_sigma.shape[1]
    cols = noise_sigma.shape[2]
    elem_rows = rows // EL
    elem_cols = cols // EL
    node_rows, node_cols, comps, width = node_panel.shape
    elements = elem_rows * elem_cols

    shapes = corner_shapes(rows, cols)
    live_rows = jnp.repeat(crack_mask.astype(jnp.float32), 128, axis=1)
    pixel_scale = live_rows[None] / noise_sigma
    design = (
        shapes[:, None, None] * pixel_scale[None, None] * coefficients.astype(jnp.float32)[None]
    ).astype(jnp.bfloat16)
    design = design.reshape(4, 3, CAMS, elem_rows, EL, elem_cols, EL).transpose(3, 5, 0, 1, 2, 4, 6)
    design = design.reshape(elements, 12, CAMS * EL * EL)
    weighted = (pixel_scale * residual).astype(jnp.bfloat16)
    weighted = weighted.reshape(CAMS, elem_rows, EL, elem_cols, EL).transpose(1, 3, 0, 2, 4)
    weighted = weighted.reshape(elements, CAMS * EL * EL)
    gram = jnp.einsum("eip,ejp->eij", design, design, preferred_element_type=jnp.float32)
    proj = jnp.einsum("eip,ep->ei", design, weighted, preferred_element_type=jnp.float32)

    payload = jnp.concatenate([node_panel.reshape(-1).astype(jnp.float32), gram.reshape(-1), proj.reshape(-1)])
    own = exchange_gather(as_lanes(payload, jnp.float32), ("row", "col"))
    own = own.reshape(tiles, -1)
    n_nodes = node_rows * node_cols * comps * width
    n_gram = elements * 144
    own_nodes = own[:, :n_nodes].reshape(n_row, n_col, node_rows, node_cols, comps, width)
    own_nodes = own_nodes.transpose(0, 2, 1, 3, 4, 5).reshape(n_row * node_rows, n_col * node_cols, comps, width)
    grams = own[:, n_nodes : n_nodes + n_gram].reshape(n_row, n_col, elem_rows, elem_cols, 12, 12)
    grams = grams.transpose(0, 2, 1, 3, 4, 5).reshape(-1, 12, 12)
    projs = own[:, n_nodes + n_gram : n_nodes + n_gram + elements * 12]
    projs = projs.reshape(n_row, n_col, elem_rows, elem_cols, 12).transpose(0, 2, 1, 3, 4).reshape(-1, 12)

    route = []
    for b in range(n_param):
        for t in range(tiles):
            route.append((b * tiles + t, (per_block * t + b % per_block) * tiles + b // per_block))
    moved = lax.ppermute(as_lanes(node_panel.reshape(-1), jnp.bfloat16), ("param", "row", "col"), route)
    cross = exchange_gather(moved, "param").reshape(n_param, -1)[:, : node_rows * node_cols * comps * width]
    cross = cross.reshape(n_row, n_col, per_block, node_rows, node_cols, comps, width)
    cross = cross.transpose(0, 3, 1, 4, 5, 2, 6)
    cross = cross.reshape(n_row * node_rows, n_col * node_cols, comps, per_block * width)

    rows_of = element_corners(own_nodes.astype(jnp.bfloat16))
    cols_of = element_corners(cross)
    weighted_rows = jnp.sum(grams.transpose(1, 2, 0)[:, :, :, None] * rows_of.astype(jnp.float32)[:, None], axis=0)
    high = lax.reduce_precision(weighted_rows, exponent_bits=8, mantissa_bits=7)
    low = weighted_rows - high
    stacked = jnp.concatenate([high.astype(jnp.bfloat16), low.astype(jnp.bfloat16)], axis=2)
    product = jnp.einsum("jep,jeq->pq", stacked, cols_of, preferred_element_type=jnp.float32)
    hessian = product[:width] + product[width:]
    gradient = jnp.einsum("iep,ie->p", rows_of.astype(jnp.float32), projs.T, precision=HIGHEST)
    share = width // tiles
    gradient = lax.dynamic_slice(gradient, (lax.axis_index(("row", "col")) * share,), (share,))
    return (hessian, gradient)


def solution(mesh):
    in_specs = (
        P(None, None, "row", "col"),
        P(None, "row", "col"),
        P(None, "row", "col"),
        P("row", "col"),
        P("row", "col", None, "param"),
    )
    out_specs = (P("param", ("row", "col")), P(("param", "row", "col")))
    return jax.shard_map(
        on_device, mesh=mesh, in_specs=in_specs, out_specs=out_specs, check_vma=False
    )
```

```python
import jax
import jax.numpy as jnp
from jax import lax
from jax.sharding import PartitionSpec as P

EL = 8
CAMS = 2
LANES = 128
HIGHEST = lax.Precision.HIGHEST

def corner_shapes(rows, cols):
    vertical = ((jnp.arange(rows) % EL).astype(jnp.float32) + 0.5) / EL
    horizontal = ((jnp.arange(cols) % EL).astype(jnp.float32) + 0.5) / EL
    lower = vertical[:, None]
    right = horizontal[None, :]
    return jnp.stack(
        [(1.0 - lower) * (1.0 - right), (1.0 - lower) * right, lower * (1.0 - right), lower * right]
    )


def exchange_gather(piece, axes):
    size = lax.axis_size(axes)
    copies = jnp.broadcast_to(piece[None], (size,) + piece.shape)
    return lax.all_to_all(copies, axes, 0, 0, tiled=False)


def as_lanes(flat, dtype):
    rows = -(-flat.shape[0] // (8 * LANES)) * 8
    flat = jnp.pad(flat.astype(dtype), (0, rows * LANES - flat.shape[0]))
    return flat.reshape(rows, LANES)


def element_corners(nodes):
    extended = jnp.pad(nodes, ((0, 1), (0, 1), (0, 0), (0, 0)))
    corners = jnp.stack(
        [extended[:-1, :-1], extended[:-1, 1:], extended[1:, :-1], extended[1:, 1:]], axis=0
    )
    corners = corners.transpose(0, 3, 1, 2, 4)
    return corners.reshape(12, nodes.shape[0] * nodes.shape[1], nodes.shape[3])


def on_device(coefficients, noise_sigma, residual, crack_mask, node_panel):
    n_param = lax.axis_size("param")
    n_row = lax.axis_size("row")
    n_col = lax.axis_size("col")
    tiles = n_row * n_col
    per_block = n_param // tiles
    rows = noise_sigma.shape[1]
    cols = noise_sigma.shape[2]
    elem_rows = rows // EL
    elem_cols = cols // EL
    node_rows, node_cols, comps, width = node_panel.shape
    elements = elem_rows * elem_cols

    shapes = corner_shapes(rows, cols)
    live_rows = jnp.repeat(crack_mask.astype(jnp.float32), 128, axis=1)
    pixel_scale = live_rows[None] / noise_sigma
    design = (
        shapes[:, None, None] * pixel_scale[None, None] * coefficients.astype(jnp.float32)[None]
    ).astype(jnp.bfloat16)
    design = design.reshape(4, 3, CAMS, elem_rows, EL, elem_cols, EL).transpose(3, 5, 0, 1, 2, 4, 6)
    design = design.reshape(elements, 12, CAMS * EL * EL)
    weighted = (pixel_scale * residual).astype(jnp.bfloat16)
    weighted = weighted.reshape(CAMS, elem_rows, EL, elem_cols, EL).transpose(1, 3, 0, 2, 4)
    weighted = weighted.reshape(elements, CAMS * EL * EL)
    gram = jnp.einsum("eip,ejp->eij", design, design, preferred_element_type=jnp.float32)
    proj = jnp.einsum("eip,ep->ei", design, weighted, preferred_element_type=jnp.float32)

    n_nodes = node_rows * node_cols * comps * width
    n_gram = elements * 144
    panel = exchange_gather(as_lanes(node_panel.reshape(-1), jnp.bfloat16), "param")
    panel = panel.reshape(n_param, -1)[:, :n_nodes]
    own_block = lax.dynamic_index_in_dim(panel, lax.axis_index("param"), axis=0, keepdims=False)
    common = jnp.concatenate([own_block.astype(jnp.float32), gram.reshape(-1), proj.reshape(-1)])
    per_tile = panel.reshape(tiles, per_block * n_nodes).astype(jnp.float32)
    chunks = jnp.concatenate([per_tile, jnp.broadcast_to(common[None], (tiles,) + common.shape)], axis=1)
    rows_used = -(-chunks.shape[1] // (8 * LANES)) * 8
    chunks = jnp.pad(chunks, ((0, 0), (0, rows_used * LANES - chunks.shape[1])))
    got = lax.all_to_all(chunks.reshape(tiles, rows_used, LANES), ("row", "col"), 0, 0, tiled=False)
    got = got.reshape(tiles, -1)
    cross = got[:, : per_block * n_nodes].astype(jnp.bfloat16)
    cross = cross.reshape(n_row, n_col, per_block, node_rows, node_cols, comps, width)
    cross = cross.transpose(0, 3, 1, 4, 5, 2, 6)
    cross = cross.reshape(n_row * node_rows, n_col * node_cols, comps, per_block * width)
    base = per_block * n_nodes
    own_nodes = got[:, base : base + n_nodes].reshape(n_row, n_col, node_rows, node_cols, comps, width)
    own_nodes = own_nodes.transpose(0, 2, 1, 3, 4, 5).reshape(n_row * node_rows, n_col * node_cols, comps, width)
    grams = got[:, base + n_nodes : base + n_nodes + n_gram].reshape(n_row, n_col, elem_rows, elem_cols, 12, 12)
    grams = grams.transpose(0, 2, 1, 3, 4, 5).reshape(-1, 12, 12)
    projs = got[:, base + n_nodes + n_gram : base + n_nodes + n_gram + elements * 12]
    projs = projs.reshape(n_row, n_col, elem_rows, elem_cols, 12).transpose(0, 2, 1, 3, 4).reshape(-1, 12)

    rows_of = element_corners(own_nodes.astype(jnp.bfloat16))
    cols_of = element_corners(cross)
    weighted_rows = jnp.sum(grams.transpose(1, 2, 0)[:, :, :, None] * rows_of.astype(jnp.float32)[:, None], axis=0)
    high = lax.reduce_precision(weighted_rows, exponent_bits=8, mantissa_bits=7)
    low = weighted_rows - high
    stacked = jnp.concatenate([high.astype(jnp.bfloat16), low.astype(jnp.bfloat16)], axis=2)
    product = jnp.einsum("jep,jeq->pq", stacked, cols_of, preferred_element_type=jnp.float32)
    hessian = product[:width] + product[width:]
    gradient = jnp.einsum("iep,ie->p", rows_of.astype(jnp.float32), projs.T, precision=HIGHEST)
    share = width // tiles
    gradient = lax.dynamic_slice(gradient, (lax.axis_index(("row", "col")) * share,), (share,))
    return (hessian, gradient)


def solution(mesh):
    in_specs = (
        P(None, None, "row", "col"),
        P(None, "row", "col"),
        P(None, "row", "col"),
        P("row", "col"),
        P("row", "col", None, "param"),
    )
    out_specs = (P("param", ("row", "col")), P(("param", "row", "col")))
    return jax.shard_map(
        on_device, mesh=mesh, in_specs=in_specs, out_specs=out_specs, check_vma=False
    )
```

```python
import jax
import jax.numpy as jnp
from jax import lax
from jax.sharding import PartitionSpec as P

EL = 8
CAMS = 2
LANES = 128
HIGHEST = lax.Precision.HIGHEST

def corner_shapes(rows, cols):
    vertical = ((jnp.arange(rows) % EL).astype(jnp.float32) + 0.5) / EL
    horizontal = ((jnp.arange(cols) % EL).astype(jnp.float32) + 0.5) / EL
    lower = vertical[:, None]
    right = horizontal[None, :]
    return jnp.stack(
        [(1.0 - lower) * (1.0 - right), (1.0 - lower) * right, lower * (1.0 - right), lower * right]
    )


def exchange_gather(piece, axes):
    size = lax.axis_size(axes)
    copies = jnp.broadcast_to(piece[None], (size,) + piece.shape)
    return lax.all_to_all(copies, axes, 0, 0, tiled=False)


def as_lanes(flat, dtype):
    rows = -(-flat.shape[0] // (8 * LANES)) * 8
    flat = jnp.pad(flat.astype(dtype), (0, rows * LANES - flat.shape[0]))
    return flat.reshape(rows, LANES)


def element_corners(nodes):
    extended = jnp.pad(nodes, ((0, 1), (0, 1), (0, 0), (0, 0)))
    corners = jnp.stack(
        [extended[:-1, :-1], extended[:-1, 1:], extended[1:, :-1], extended[1:, 1:]], axis=0
    )
    corners = corners.transpose(0, 3, 1, 2, 4)
    return corners.reshape(12, nodes.shape[0] * nodes.shape[1], nodes.shape[3])


def on_device(coefficients, noise_sigma, residual, crack_mask, node_panel):
    n_param = lax.axis_size("param")
    n_row = lax.axis_size("row")
    n_col = lax.axis_size("col")
    tiles = n_row * n_col
    per_block = n_param // tiles
    rows = noise_sigma.shape[1]
    cols = noise_sigma.shape[2]
    elem_rows = rows // EL
    elem_cols = cols // EL
    node_rows, node_cols, comps, width = node_panel.shape
    elements = elem_rows * elem_cols

    shapes = corner_shapes(rows, cols)
    live_rows = jnp.repeat(crack_mask.astype(jnp.float32), 128, axis=1)
    pixel_scale = live_rows[None] / noise_sigma
    design = (
        shapes[:, None, None] * pixel_scale[None, None] * coefficients.astype(jnp.float32)[None]
    ).astype(jnp.bfloat16)
    design = design.reshape(4, 3, CAMS, elem_rows, EL, elem_cols, EL).transpose(3, 5, 0, 1, 2, 4, 6)
    design = design.reshape(elements, 12, CAMS * EL * EL)
    weighted = (pixel_scale * residual).astype(jnp.bfloat16)
    weighted = weighted.reshape(CAMS, elem_rows, EL, elem_cols, EL).transpose(1, 3, 0, 2, 4)
    weighted = weighted.reshape(elements, CAMS * EL * EL)
    gram = jnp.einsum("eip,ejp->eij", design, design, preferred_element_type=jnp.float32)
    proj = jnp.einsum("eip,ep->ei", design, weighted, preferred_element_type=jnp.float32)

    payload = jnp.concatenate([node_panel.reshape(-1).astype(jnp.float32), gram.reshape(-1), proj.reshape(-1)])
    own = exchange_gather(as_lanes(payload, jnp.float32), ("row", "col"))
    own = own.reshape(tiles, -1)
    n_nodes = node_rows * node_cols * comps * width
    n_gram = elements * 144
    own_nodes = own[:, :n_nodes].reshape(n_row, n_col, node_rows, node_cols, comps, width)
    own_nodes = own_nodes.transpose(0, 2, 1, 3, 4, 5).reshape(n_row * node_rows, n_col * node_cols, comps, width)
    grams = own[:, n_nodes : n_nodes + n_gram].reshape(n_row, n_col, elem_rows, elem_cols, 12, 12)
    grams = grams.transpose(0, 2, 1, 3, 4, 5).reshape(-1, 12, 12)
    projs = own[:, n_nodes + n_gram : n_nodes + n_gram + elements * 12]
    projs = projs.reshape(n_row, n_col, elem_rows, elem_cols, 12).transpose(0, 2, 1, 3, 4).reshape(-1, 12)

    half = n_param // 2
    pieces = []
    for flip in (0, half):
        route = []
        for b in range(n_param):
            for t in range(tiles):
                target = (per_block * t + b % per_block) ^ flip
                route.append((b * tiles + t, target * tiles + b // per_block))
        pieces.append(lax.ppermute(as_lanes(node_panel.reshape(-1), jnp.bfloat16), ("param", "row", "col"), route))
    pair = jnp.stack(pieces)
    groups = [list(range(half)), list(range(half, n_param))]
    copies = jnp.broadcast_to(pair[None], (half,) + pair.shape)
    got = lax.all_to_all(copies, "param", 0, 0, axis_index_groups=groups, tiled=False)
    upper = lax.axis_index("param") // half
    got = jnp.where(upper == 0, got, got[:, ::-1])
    cross = got.transpose(1, 0, 2, 3).reshape(n_param, -1)[:, : node_rows * node_cols * comps * width]
    cross = cross.reshape(n_row, n_col, per_block, node_rows, node_cols, comps, width)
    cross = cross.transpose(0, 3, 1, 4, 5, 2, 6)
    cross = cross.reshape(n_row * node_rows, n_col * node_cols, comps, per_block * width)

    rows_of = element_corners(own_nodes.astype(jnp.bfloat16))
    cols_of = element_corners(cross)
    weighted_rows = jnp.sum(grams.transpose(1, 2, 0)[:, :, :, None] * rows_of.astype(jnp.float32)[:, None], axis=0)
    high = lax.reduce_precision(weighted_rows, exponent_bits=8, mantissa_bits=7)
    low = weighted_rows - high
    stacked = jnp.concatenate([high.astype(jnp.bfloat16), low.astype(jnp.bfloat16)], axis=2)
    product = jnp.einsum("jep,jeq->pq", stacked, cols_of, preferred_element_type=jnp.float32)
    hessian = product[:width] + product[width:]
    gradient = jnp.einsum("iep,ie->p", rows_of.astype(jnp.float32), projs.T, precision=HIGHEST)
    share = width // tiles
    gradient = lax.dynamic_slice(gradient, (lax.axis_index(("row", "col")) * share,), (share,))
    return (hessian, gradient)


def solution(mesh):
    in_specs = (
        P(None, None, "row", "col"),
        P(None, "row", "col"),
        P(None, "row", "col"),
        P("row", "col"),
        P("row", "col", None, "param"),
    )
    out_specs = (P("param", ("row", "col")), P(("param", "row", "col")))
    return jax.shard_map(
        on_device, mesh=mesh, in_specs=in_specs, out_specs=out_specs, check_vma=False
    )
```

```python
import jax
import jax.numpy as jnp
import numpy as np
from jax import lax
from jax.sharding import PartitionSpec as P

EL = 8
CAMS = 2
LANES = 128
HIGHEST = lax.Precision.HIGHEST

def corner_shapes(rows, cols):
    vertical = ((jnp.arange(rows) % EL).astype(jnp.float32) + 0.5) / EL
    horizontal = ((jnp.arange(cols) % EL).astype(jnp.float32) + 0.5) / EL
    lower = vertical[:, None]
    right = horizontal[None, :]
    return jnp.stack(
        [(1.0 - lower) * (1.0 - right), (1.0 - lower) * right, lower * (1.0 - right), lower * right]
    )


def exchange_gather(piece, axes):
    size = lax.axis_size(axes)
    copies = jnp.broadcast_to(piece[None], (size,) + piece.shape)
    return lax.all_to_all(copies, axes, 0, 0, tiled=False)


def as_lanes(flat, dtype):
    rows = -(-flat.shape[0] // (8 * LANES)) * 8
    flat = jnp.pad(flat.astype(dtype), (0, rows * LANES - flat.shape[0]))
    return flat.reshape(rows, LANES)


def element_corners(nodes):
    extended = jnp.pad(nodes, ((0, 1), (0, 1), (0, 0), (0, 0)))
    corners = jnp.stack(
        [extended[:-1, :-1], extended[:-1, 1:], extended[1:, :-1], extended[1:, 1:]], axis=0
    )
    corners = corners.transpose(0, 3, 1, 2, 4)
    return corners.reshape(12, nodes.shape[0] * nodes.shape[1], nodes.shape[3])


def on_device(coefficients, noise_sigma, residual, crack_mask, node_panel):
    n_param = lax.axis_size("param")
    n_row = lax.axis_size("row")
    n_col = lax.axis_size("col")
    tiles = n_row * n_col
    per_block = n_param // tiles
    rows = noise_sigma.shape[1]
    cols = noise_sigma.shape[2]
    elem_rows = rows // EL
    elem_cols = cols // EL
    node_rows, node_cols, comps, width = node_panel.shape
    elements = elem_rows * elem_cols

    shapes = corner_shapes(rows, cols)
    live_rows = jnp.repeat(crack_mask.astype(jnp.float32), 128, axis=1)
    pixel_scale = live_rows[None] / noise_sigma
    design = (
        shapes[:, None, None] * pixel_scale[None, None] * coefficients.astype(jnp.float32)[None]
    ).astype(jnp.bfloat16)
    design = design.reshape(4, 3, CAMS, elem_rows, EL, elem_cols, EL).transpose(3, 5, 0, 1, 2, 4, 6)
    design = design.reshape(elements, 12, CAMS * EL * EL)
    weighted = (pixel_scale * residual).astype(jnp.bfloat16)
    weighted = weighted.reshape(CAMS, elem_rows, EL, elem_cols, EL).transpose(1, 3, 0, 2, 4)
    weighted = weighted.reshape(elements, CAMS * EL * EL)
    gram = jnp.einsum("eip,ejp->eij", design, design, preferred_element_type=jnp.float32)
    proj = jnp.einsum("eip,ep->ei", design, weighted, preferred_element_type=jnp.float32)

    upper_i, upper_j = np.triu_indices(12)
    full_index = np.zeros((12, 12), np.int32)
    full_index[upper_i, upper_j] = np.arange(upper_i.size)
    full_index[upper_j, upper_i] = np.arange(upper_i.size)
    floats = jnp.concatenate([gram[:, upper_i, upper_j].reshape(-1), proj.reshape(-1)])
    high = lax.reduce_precision(floats, exponent_bits=8, mantissa_bits=7)
    low = floats - high
    payload = jnp.concatenate(
        [node_panel.reshape(-1), high.astype(jnp.bfloat16), low.astype(jnp.bfloat16)]
    )
    own = exchange_gather(as_lanes(payload, jnp.bfloat16), ("row", "col"))
    own = own.reshape(tiles, -1)
    n_nodes = node_rows * node_cols * comps * width
    n_floats = elements * upper_i.size + elements * 12
    own_nodes = own[:, :n_nodes].reshape(n_row, n_col, node_rows, node_cols, comps, width)
    own_nodes = own_nodes.transpose(0, 2, 1, 3, 4, 5).reshape(n_row * node_rows, n_col * node_cols, comps, width)
    floats = own[:, n_nodes : n_nodes + n_floats].astype(jnp.float32)
    floats = floats + own[:, n_nodes + n_floats : n_nodes + 2 * n_floats].astype(jnp.float32)
    n_upper = elements * upper_i.size
    grams = floats[:, :n_upper].reshape(n_row, n_col, elem_rows, elem_cols, upper_i.size)
    grams = grams.transpose(0, 2, 1, 3, 4).reshape(-1, upper_i.size)[:, full_index]
    projs = floats[:, n_upper:].reshape(n_row, n_col, elem_rows, elem_cols, 12)
    projs = projs.transpose(0, 2, 1, 3, 4).reshape(-1, 12)

    route = []
    for b in range(n_param):
        for t in range(tiles):
            route.append((b * tiles + t, (per_block * t + b % per_block) * tiles + b // per_block))
    moved = lax.ppermute(as_lanes(node_panel.reshape(-1), jnp.bfloat16), ("param", "row", "col"), route)
    cross = exchange_gather(moved, "param").reshape(n_param, -1)[:, : node_rows * node_cols * comps * width]
    cross = cross.reshape(n_row, n_col, per_block, node_rows, node_cols, comps, width)
    cross = cross.transpose(0, 3, 1, 4, 5, 2, 6)
    cross = cross.reshape(n_row * node_rows, n_col * node_cols, comps, per_block * width)

    rows_of = element_corners(own_nodes.astype(jnp.bfloat16))
    cols_of = element_corners(cross)
    weighted_rows = jnp.sum(grams.transpose(1, 2, 0)[:, :, :, None] * rows_of.astype(jnp.float32)[:, None], axis=0)
    high = lax.reduce_precision(weighted_rows, exponent_bits=8, mantissa_bits=7)
    low = weighted_rows - high
    stacked = jnp.concatenate([high.astype(jnp.bfloat16), low.astype(jnp.bfloat16)], axis=2)
    product = jnp.einsum("jep,jeq->pq", stacked, cols_of, preferred_element_type=jnp.float32)
    hessian = product[:width] + product[width:]
    gradient = jnp.einsum("iep,ie->p", rows_of.astype(jnp.float32), projs.T, precision=HIGHEST)
    share = width // tiles
    gradient = lax.dynamic_slice(gradient, (lax.axis_index(("row", "col")) * share,), (share,))
    return (hessian, gradient)


def solution(mesh):
    in_specs = (
        P(None, None, "row", "col"),
        P(None, "row", "col"),
        P(None, "row", "col"),
        P("row", "col"),
        P("row", "col", None, "param"),
    )
    out_specs = (P("param", ("row", "col")), P(("param", "row", "col")))
    return jax.shard_map(
        on_device, mesh=mesh, in_specs=in_specs, out_specs=out_specs, check_vma=False
    )
```

```python
import jax
import jax.numpy as jnp
import numpy as np
from jax import lax
from jax.sharding import PartitionSpec as P

EL = 8
CAMS = 2
LANES = 128
HIGHEST = lax.Precision.HIGHEST

def corner_shapes(rows, cols):
    vertical = ((jnp.arange(rows) % EL).astype(jnp.float32) + 0.5) / EL
    horizontal = ((jnp.arange(cols) % EL).astype(jnp.float32) + 0.5) / EL
    lower = vertical[:, None]
    right = horizontal[None, :]
    return jnp.stack(
        [(1.0 - lower) * (1.0 - right), (1.0 - lower) * right, lower * (1.0 - right), lower * right]
    )


def exchange_gather(piece, axes):
    size = lax.axis_size(axes)
    copies = jnp.broadcast_to(piece[None], (size,) + piece.shape)
    return lax.all_to_all(copies, axes, 0, 0, tiled=False)


def ring_distance(a, b, n):
    d = abs(a - b) % n
    return min(d, n - d)


def landing_places(n_param, n_row, n_col, per_block):
    z_size = n_param // 2
    tiles = n_row * n_col

    def hops(t, j, T, a):
        b = per_block * T + j
        dz = ring_distance(a % z_size, b % z_size, z_size)
        dx = ring_distance(t // n_col, T // n_col, n_row)
        y_from = 2 * ((t % n_col) // 2) + b // z_size
        y_to = 2 * ((T % n_col) // 2) + a // z_size
        return dz + dx + ring_distance(y_from, y_to, 4)

    table = np.zeros((tiles, tiles * per_block), np.int32)
    for T in range(tiles):
        sources = [(t, j) for t in range(tiles) for j in range(per_block)]
        sources.sort(key=lambda s: -(ring_distance(s[0] // n_col, T // n_col, n_row)
                                     + 2 * ring_distance((s[0] % n_col) // 2, (T % n_col) // 2, 2)))
        free = list(range(n_param))
        for t, j in sources:
            place = min(free, key=lambda a: (hops(t, j, T, a), a))
            free.remove(place)
            table[T, t * per_block + j] = place
    return table


def as_lanes(flat, dtype):
    rows = -(-flat.shape[0] // (8 * LANES)) * 8
    flat = jnp.pad(flat.astype(dtype), (0, rows * LANES - flat.shape[0]))
    return flat.reshape(rows, LANES)


def element_corners(nodes):
    extended = jnp.pad(nodes, ((0, 1), (0, 1), (0, 0), (0, 0)))
    corners = jnp.stack(
        [extended[:-1, :-1], extended[:-1, 1:], extended[1:, :-1], extended[1:, 1:]], axis=0
    )
    corners = corners.transpose(0, 3, 1, 2, 4)
    return corners.reshape(12, nodes.shape[0] * nodes.shape[1], nodes.shape[3])


def on_device(coefficients, noise_sigma, residual, crack_mask, node_panel):
    n_param = lax.axis_size("param")
    n_row = lax.axis_size("row")
    n_col = lax.axis_size("col")
    tiles = n_row * n_col
    per_block = n_param // tiles
    rows = noise_sigma.shape[1]
    cols = noise_sigma.shape[2]
    elem_rows = rows // EL
    elem_cols = cols // EL
    node_rows, node_cols, comps, width = node_panel.shape
    elements = elem_rows * elem_cols

    shapes = corner_shapes(rows, cols)
    live_rows = jnp.repeat(crack_mask.astype(jnp.float32), 128, axis=1)
    pixel_scale = live_rows[None] / noise_sigma
    design = (
        shapes[:, None, None] * pixel_scale[None, None] * coefficients.astype(jnp.float32)[None]
    ).astype(jnp.bfloat16)
    design = design.reshape(4, 3, CAMS, elem_rows, EL, elem_cols, EL).transpose(3, 5, 0, 1, 2, 4, 6)
    design = design.reshape(elements, 12, CAMS * EL * EL)
    weighted = (pixel_scale * residual).astype(jnp.bfloat16)
    weighted = weighted.reshape(CAMS, elem_rows, EL, elem_cols, EL).transpose(1, 3, 0, 2, 4)
    weighted = weighted.reshape(elements, CAMS * EL * EL)
    gram = jnp.einsum("eip,ejp->eij", design, design, preferred_element_type=jnp.float32)
    proj = jnp.einsum("eip,ep->ei", design, weighted, preferred_element_type=jnp.float32)

    payload = jnp.concatenate([node_panel.reshape(-1).astype(jnp.float32), gram.reshape(-1), proj.reshape(-1)])
    own = exchange_gather(as_lanes(payload, jnp.float32), ("row", "col"))
    own = own.reshape(tiles, -1)
    n_nodes = node_rows * node_cols * comps * width
    n_gram = elements * 144
    own_nodes = own[:, :n_nodes].reshape(n_row, n_col, node_rows, node_cols, comps, width)
    own_nodes = own_nodes.transpose(0, 2, 1, 3, 4, 5).reshape(n_row * node_rows, n_col * node_cols, comps, width)
    grams = own[:, n_nodes : n_nodes + n_gram].reshape(n_row, n_col, elem_rows, elem_cols, 12, 12)
    grams = grams.transpose(0, 2, 1, 3, 4, 5).reshape(-1, 12, 12)
    projs = own[:, n_nodes + n_gram : n_nodes + n_gram + elements * 12]
    projs = projs.reshape(n_row, n_col, elem_rows, elem_cols, 12).transpose(0, 2, 1, 3, 4).reshape(-1, 12)

    places = landing_places(n_param, n_row, n_col, per_block)
    route = []
    for b in range(n_param):
        for t in range(tiles):
            T = b // per_block
            route.append((b * tiles + t, int(places[T, t * per_block + b % per_block]) * tiles + T))
    moved = lax.ppermute(as_lanes(node_panel.reshape(-1), jnp.bfloat16), ("param", "row", "col"), route)
    cross = exchange_gather(moved, "param")
    cross = jnp.take(cross, jnp.asarray(places)[lax.axis_index(("row", "col"))], axis=0)
    cross = cross.reshape(n_param, -1)[:, : node_rows * node_cols * comps * width]
    cross = cross.reshape(n_row, n_col, per_block, node_rows, node_cols, comps, width)
    cross = cross.transpose(0, 3, 1, 4, 5, 2, 6)
    cross = cross.reshape(n_row * node_rows, n_col * node_cols, comps, per_block * width)

    rows_of = element_corners(own_nodes.astype(jnp.bfloat16))
    cols_of = element_corners(cross)
    weighted_rows = jnp.sum(grams.transpose(1, 2, 0)[:, :, :, None] * rows_of.astype(jnp.float32)[:, None], axis=0)
    high = lax.reduce_precision(weighted_rows, exponent_bits=8, mantissa_bits=7)
    low = weighted_rows - high
    stacked = jnp.concatenate([high.astype(jnp.bfloat16), low.astype(jnp.bfloat16)], axis=2)
    product = jnp.einsum("jep,jeq->pq", stacked, cols_of, preferred_element_type=jnp.float32)
    hessian = product[:width] + product[width:]
    gradient = jnp.einsum("iep,ie->p", rows_of.astype(jnp.float32), projs.T, precision=HIGHEST)
    share = width // tiles
    gradient = lax.dynamic_slice(gradient, (lax.axis_index(("row", "col")) * share,), (share,))
    return (hessian, gradient)


def solution(mesh):
    in_specs = (
        P(None, None, "row", "col"),
        P(None, "row", "col"),
        P(None, "row", "col"),
        P("row", "col"),
        P("row", "col", None, "param"),
    )
    out_specs = (P("param", ("row", "col")), P(("param", "row", "col")))
    return jax.shard_map(
        on_device, mesh=mesh, in_specs=in_specs, out_specs=out_specs, check_vma=False
    )
```

```python
import jax
import jax.numpy as jnp
import numpy as np
from jax import lax
from jax.sharding import PartitionSpec as P

EL = 8
CAMS = 2
LANES = 128
HIGHEST = lax.Precision.HIGHEST

def corner_shapes(rows, cols):
    vertical = ((jnp.arange(rows) % EL).astype(jnp.float32) + 0.5) / EL
    horizontal = ((jnp.arange(cols) % EL).astype(jnp.float32) + 0.5) / EL
    lower = vertical[:, None]
    right = horizontal[None, :]
    return jnp.stack(
        [(1.0 - lower) * (1.0 - right), (1.0 - lower) * right, lower * (1.0 - right), lower * right]
    )


def exchange_gather(piece, axes):
    size = lax.axis_size(axes)
    copies = jnp.broadcast_to(piece[None], (size,) + piece.shape)
    return lax.all_to_all(copies, axes, 0, 0, tiled=False)


def ring_distance(a, b, n):
    d = abs(a - b) % n
    return min(d, n - d)


def landing_places(n_param, n_row, n_col, per_block):
    z_size = n_param // 2
    tiles = n_row * n_col

    def hops(t, j, T, a):
        b = per_block * T + j
        dz = ring_distance(a % z_size, b % z_size, z_size)
        dx = ring_distance(t // n_col, T // n_col, n_row)
        y_from = 2 * ((t % n_col) // 2) + b // z_size
        y_to = 2 * ((T % n_col) // 2) + a // z_size
        return dz + dx + ring_distance(y_from, y_to, 4)

    table = np.zeros((tiles, tiles * per_block), np.int32)
    for T in range(tiles):
        sources = [(t, j) for t in range(tiles) for j in range(per_block)]
        sources.sort(key=lambda s: -(ring_distance(s[0] // n_col, T // n_col, n_row)
                                     + 2 * ring_distance((s[0] % n_col) // 2, (T % n_col) // 2, 2)))
        free = list(range(n_param))
        for t, j in sources:
            place = min(free, key=lambda a: (hops(t, j, T, a), a))
            free.remove(place)
            table[T, t * per_block + j] = place
    return table


def as_lanes(flat, dtype):
    rows = -(-flat.shape[0] // (8 * LANES)) * 8
    flat = jnp.pad(flat.astype(dtype), (0, rows * LANES - flat.shape[0]))
    return flat.reshape(rows, LANES)


def element_corners(nodes):
    extended = jnp.pad(nodes, ((0, 1), (0, 1), (0, 0), (0, 0)))
    corners = jnp.stack(
        [extended[:-1, :-1], extended[:-1, 1:], extended[1:, :-1], extended[1:, 1:]], axis=0
    )
    corners = corners.transpose(0, 3, 1, 2, 4)
    return corners.reshape(12, nodes.shape[0] * nodes.shape[1], nodes.shape[3])


def on_device(coefficients, noise_sigma, residual, crack_mask, node_panel):
    n_param = lax.axis_size("param")
    n_row = lax.axis_size("row")
    n_col = lax.axis_size("col")
    tiles = n_row * n_col
    per_block = n_param // tiles
    rows = noise_sigma.shape[1]
    cols = noise_sigma.shape[2]
    elem_rows = rows // EL
    elem_cols = cols // EL
    node_rows, node_cols, comps, width = node_panel.shape
    elements = elem_rows * elem_cols

    shapes = corner_shapes(rows, cols)
    live_rows = jnp.repeat(crack_mask.astype(jnp.float32), 128, axis=1)
    pixel_scale = live_rows[None] / noise_sigma
    design = (
        shapes[:, None, None] * pixel_scale[None, None] * coefficients.astype(jnp.float32)[None]
    ).astype(jnp.bfloat16)
    design = design.reshape(4, 3, CAMS, elem_rows, EL, elem_cols, EL).transpose(3, 5, 0, 1, 2, 4, 6)
    design = design.reshape(elements, 12, CAMS * EL * EL)
    weighted = (pixel_scale * residual).astype(jnp.bfloat16)
    weighted = weighted.reshape(CAMS, elem_rows, EL, elem_cols, EL).transpose(1, 3, 0, 2, 4)
    weighted = weighted.reshape(elements, CAMS * EL * EL)
    gram = jnp.einsum("eip,ejp->eij", design, design, preferred_element_type=jnp.float32)
    proj = jnp.einsum("eip,ep->ei", design, weighted, preferred_element_type=jnp.float32)

    places = landing_places(n_param, n_row, n_col, per_block)
    route = []
    for b in range(n_param):
        for t in range(tiles):
            T = b // per_block
            route.append((b * tiles + t, int(places[T, t * per_block + b % per_block]) * tiles + T))
    moved = lax.ppermute(as_lanes(node_panel.reshape(-1), jnp.bfloat16), ("param", "row", "col"), route)
    payload = jnp.concatenate([node_panel.reshape(-1).astype(jnp.float32), gram.reshape(-1), proj.reshape(-1)])
    lanes, moved = lax.optimization_barrier((as_lanes(payload, jnp.float32), moved))
    own = exchange_gather(lanes, ("row", "col"))
    own = own.reshape(tiles, -1)
    n_nodes = node_rows * node_cols * comps * width
    n_gram = elements * 144
    own_nodes = own[:, :n_nodes].reshape(n_row, n_col, node_rows, node_cols, comps, width)
    own_nodes = own_nodes.transpose(0, 2, 1, 3, 4, 5).reshape(n_row * node_rows, n_col * node_cols, comps, width)
    grams = own[:, n_nodes : n_nodes + n_gram].reshape(n_row, n_col, elem_rows, elem_cols, 12, 12)
    grams = grams.transpose(0, 2, 1, 3, 4, 5).reshape(-1, 12, 12)
    projs = own[:, n_nodes + n_gram : n_nodes + n_gram + elements * 12]
    projs = projs.reshape(n_row, n_col, elem_rows, elem_cols, 12).transpose(0, 2, 1, 3, 4).reshape(-1, 12)

    cross = exchange_gather(moved, "param")
    cross = jnp.take(cross, jnp.asarray(places)[lax.axis_index(("row", "col"))], axis=0)
    cross = cross.reshape(n_param, -1)[:, : node_rows * node_cols * comps * width]
    cross = cross.reshape(n_row, n_col, per_block, node_rows, node_cols, comps, width)
    cross = cross.transpose(0, 3, 1, 4, 5, 2, 6)
    cross = cross.reshape(n_row * node_rows, n_col * node_cols, comps, per_block * width)

    rows_of = element_corners(own_nodes.astype(jnp.bfloat16))
    cols_of = element_corners(cross)
    weighted_rows = jnp.sum(grams.transpose(1, 2, 0)[:, :, :, None] * rows_of.astype(jnp.float32)[:, None], axis=0)
    high = lax.reduce_precision(weighted_rows, exponent_bits=8, mantissa_bits=7)
    low = weighted_rows - high
    stacked = jnp.concatenate([high.astype(jnp.bfloat16), low.astype(jnp.bfloat16)], axis=2)
    product = jnp.einsum("jep,jeq->pq", stacked, cols_of, preferred_element_type=jnp.float32)
    hessian = product[:width] + product[width:]
    gradient = jnp.einsum("iep,ie->p", rows_of.astype(jnp.float32), projs.T, precision=HIGHEST)
    share = width // tiles
    gradient = lax.dynamic_slice(gradient, (lax.axis_index(("row", "col")) * share,), (share,))
    return (hessian, gradient)


def solution(mesh):
    in_specs = (
        P(None, None, "row", "col"),
        P(None, "row", "col"),
        P(None, "row", "col"),
        P("row", "col"),
        P("row", "col", None, "param"),
    )
    out_specs = (P("param", ("row", "col")), P(("param", "row", "col")))
    return jax.shard_map(
        on_device, mesh=mesh, in_specs=in_specs, out_specs=out_specs, check_vma=False
    )
```

```python
import jax
import jax.numpy as jnp
import numpy as np
from jax import lax
from jax.sharding import PartitionSpec as P

EL = 8
CAMS = 2
LANES = 128
HIGHEST = lax.Precision.HIGHEST

def corner_shapes(rows, cols):
    vertical = ((jnp.arange(rows) % EL).astype(jnp.float32) + 0.5) / EL
    horizontal = ((jnp.arange(cols) % EL).astype(jnp.float32) + 0.5) / EL
    lower = vertical[:, None]
    right = horizontal[None, :]
    return jnp.stack(
        [(1.0 - lower) * (1.0 - right), (1.0 - lower) * right, lower * (1.0 - right), lower * right]
    )


def exchange_gather(piece, axes):
    size = lax.axis_size(axes)
    copies = jnp.broadcast_to(piece[None], (size,) + piece.shape)
    return lax.all_to_all(copies, axes, 0, 0, tiled=False)


def ring_distance(a, b, n):
    d = abs(a - b) % n
    return min(d, n - d)


def landing_places(n_param, n_row, n_col, per_block):
    z_size = n_param // 2
    tiles = n_row * n_col

    def hops(t, j, T, a):
        b = per_block * T + j
        dz = ring_distance(a % z_size, b % z_size, z_size)
        dx = ring_distance(t // n_col, T // n_col, n_row)
        y_from = 2 * ((t % n_col) // 2) + b // z_size
        y_to = 2 * ((T % n_col) // 2) + a // z_size
        return dz + dx + ring_distance(y_from, y_to, 4)

    table = np.zeros((tiles, tiles * per_block), np.int32)
    for T in range(tiles):
        sources = [(t, j) for t in range(tiles) for j in range(per_block)]
        sources.sort(key=lambda s: -(ring_distance(s[0] // n_col, T // n_col, n_row)
                                     + 2 * ring_distance((s[0] % n_col) // 2, (T % n_col) // 2, 2)))
        free = list(range(n_param))
        for t, j in sources:
            place = min(free, key=lambda a: (hops(t, j, T, a), a))
            free.remove(place)
            table[T, t * per_block + j] = place
    return table


def as_lanes(flat, dtype):
    rows = -(-flat.shape[0] // (8 * LANES)) * 8
    flat = jnp.pad(flat.astype(dtype), (0, rows * LANES - flat.shape[0]))
    return flat.reshape(rows, LANES)


def element_corners(nodes):
    extended = jnp.pad(nodes, ((0, 1), (0, 1), (0, 0), (0, 0)))
    corners = jnp.stack(
        [extended[:-1, :-1], extended[:-1, 1:], extended[1:, :-1], extended[1:, 1:]], axis=0
    )
    corners = corners.transpose(0, 3, 1, 2, 4)
    return corners.reshape(12, nodes.shape[0] * nodes.shape[1], nodes.shape[3])


def on_device(coefficients, noise_sigma, residual, crack_mask, node_panel):
    n_param = lax.axis_size("param")
    n_row = lax.axis_size("row")
    n_col = lax.axis_size("col")
    tiles = n_row * n_col
    per_block = n_param // tiles
    rows = noise_sigma.shape[1]
    cols = noise_sigma.shape[2]
    elem_rows = rows // EL
    elem_cols = cols // EL
    node_rows, node_cols, comps, width = node_panel.shape
    elements = elem_rows * elem_cols

    shapes = corner_shapes(rows, cols)
    live_rows = jnp.repeat(crack_mask.astype(jnp.float32), 128, axis=1)
    pixel_scale = live_rows[None] / noise_sigma
    design = (
        shapes[:, None, None] * pixel_scale[None, None] * coefficients.astype(jnp.float32)[None]
    ).astype(jnp.bfloat16)
    design = design.reshape(4, 3, CAMS, elem_rows, EL, elem_cols, EL).transpose(3, 5, 0, 1, 2, 4, 6)
    design = design.reshape(elements, 12, CAMS * EL * EL)
    weighted = (pixel_scale * residual).astype(jnp.bfloat16)
    weighted = weighted.reshape(CAMS, elem_rows, EL, elem_cols, EL).transpose(1, 3, 0, 2, 4)
    weighted = weighted.reshape(elements, CAMS * EL * EL)
    gram = jnp.einsum("eip,ejp->eij", design, design, preferred_element_type=jnp.float32)
    proj = jnp.einsum("eip,ep->ei", design, weighted, preferred_element_type=jnp.float32)

    payload = jnp.concatenate([node_panel.reshape(-1).astype(jnp.float32), gram.reshape(-1), proj.reshape(-1)])
    own = exchange_gather(as_lanes(payload, jnp.float32), ("row", "col"))
    own = own.reshape(tiles, -1)
    n_nodes = node_rows * node_cols * comps * width
    n_gram = elements * 144
    own_nodes = own[:, :n_nodes].reshape(n_row, n_col, node_rows, node_cols, comps, width)
    own_nodes = own_nodes.transpose(0, 2, 1, 3, 4, 5).reshape(n_row * node_rows, n_col * node_cols, comps, width)
    grams = own[:, n_nodes : n_nodes + n_gram].reshape(n_row, n_col, elem_rows, elem_cols, 12, 12)
    grams = grams.transpose(0, 2, 1, 3, 4, 5).reshape(-1, 12, 12)
    projs = own[:, n_nodes + n_gram : n_nodes + n_gram + elements * 12]
    projs = projs.reshape(n_row, n_col, elem_rows, elem_cols, 12).transpose(0, 2, 1, 3, 4).reshape(-1, 12)

    places = landing_places(n_param, n_row, n_col, per_block)
    route = []
    for b in range(n_param):
        for t in range(tiles):
            T = b // per_block
            route.append((b * tiles + t, int(places[T, t * per_block + b % per_block]) * tiles + T))
    moved = lax.ppermute(as_lanes(node_panel.reshape(-1), jnp.bfloat16), ("param", "row", "col"), route)
    cross = exchange_gather(moved, "param")
    picks = jnp.asarray(places)[lax.axis_index(("row", "col"))]
    select = (picks[:, None] == jnp.arange(n_param)[None, :]).astype(jnp.bfloat16)
    cross = jnp.einsum("ka,ar->kr", select, cross.reshape(n_param, -1), preferred_element_type=jnp.float32)
    cross = cross.astype(jnp.bfloat16)[:, : node_rows * node_cols * comps * width]
    cross = cross.reshape(n_row, n_col, per_block, node_rows, node_cols, comps, width)
    cross = cross.transpose(0, 3, 1, 4, 5, 2, 6)
    cross = cross.reshape(n_row * node_rows, n_col * node_cols, comps, per_block * width)

    rows_of = element_corners(own_nodes.astype(jnp.bfloat16))
    cols_of = element_corners(cross)
    weighted_rows = jnp.sum(grams.transpose(1, 2, 0)[:, :, :, None] * rows_of.astype(jnp.float32)[:, None], axis=0)
    high = lax.reduce_precision(weighted_rows, exponent_bits=8, mantissa_bits=7)
    low = weighted_rows - high
    stacked = jnp.concatenate([high.astype(jnp.bfloat16), low.astype(jnp.bfloat16)], axis=2)
    product = jnp.einsum("jep,jeq->pq", stacked, cols_of, preferred_element_type=jnp.float32)
    hessian = product[:width] + product[width:]
    gradient = jnp.einsum("iep,ie->p", rows_of.astype(jnp.float32), projs.T, precision=HIGHEST)
    share = width // tiles
    gradient = lax.dynamic_slice(gradient, (lax.axis_index(("row", "col")) * share,), (share,))
    return (hessian, gradient)


def solution(mesh):
    in_specs = (
        P(None, None, "row", "col"),
        P(None, "row", "col"),
        P(None, "row", "col"),
        P("row", "col"),
        P("row", "col", None, "param"),
    )
    out_specs = (P("param", ("row", "col")), P(("param", "row", "col")))
    return jax.shard_map(
        on_device, mesh=mesh, in_specs=in_specs, out_specs=out_specs, check_vma=False
    )
```

```python
import jax
import jax.numpy as jnp
import numpy as np
from jax import lax
from jax.sharding import PartitionSpec as P

EL = 8
CAMS = 2
LANES = 128
HIGHEST = lax.Precision.HIGHEST

def corner_shapes(rows, cols):
    vertical = ((jnp.arange(rows) % EL).astype(jnp.float32) + 0.5) / EL
    horizontal = ((jnp.arange(cols) % EL).astype(jnp.float32) + 0.5) / EL
    lower = vertical[:, None]
    right = horizontal[None, :]
    return jnp.stack(
        [(1.0 - lower) * (1.0 - right), (1.0 - lower) * right, lower * (1.0 - right), lower * right]
    )


def exchange_gather(piece, axes):
    size = lax.axis_size(axes)
    copies = jnp.broadcast_to(piece[None], (size,) + piece.shape)
    return lax.all_to_all(copies, axes, 0, 0, tiled=False)


def ring_distance(a, b, n):
    d = abs(a - b) % n
    return min(d, n - d)


def landing_places(n_param, n_row, n_col, per_block):
    z_size = n_param // 2
    tiles = n_row * n_col

    def hops(t, j, T, a):
        b = per_block * T + j
        dz = ring_distance(a % z_size, b % z_size, z_size)
        dx = ring_distance(t // n_col, T // n_col, n_row)
        y_from = 2 * ((t % n_col) // 2) + b // z_size
        y_to = 2 * ((T % n_col) // 2) + a // z_size
        return dz + dx + ring_distance(y_from, y_to, 4)

    table = np.zeros((tiles, tiles * per_block), np.int32)
    for T in range(tiles):
        sources = [(t, j) for t in range(tiles) for j in range(per_block)]
        sources.sort(key=lambda s: -(ring_distance(s[0] // n_col, T // n_col, n_row)
                                     + 2 * ring_distance((s[0] % n_col) // 2, (T % n_col) // 2, 2)))
        free = list(range(n_param))
        for t, j in sources:
            place = min(free, key=lambda a: (hops(t, j, T, a), a))
            free.remove(place)
            table[T, t * per_block + j] = place
    return table


def as_lanes(flat, dtype):
    rows = -(-flat.shape[0] // (8 * LANES)) * 8
    flat = jnp.pad(flat.astype(dtype), (0, rows * LANES - flat.shape[0]))
    return flat.reshape(rows, LANES)


def element_corners(nodes):
    extended = jnp.pad(nodes, ((0, 1), (0, 1), (0, 0), (0, 0)))
    corners = jnp.stack(
        [extended[:-1, :-1], extended[:-1, 1:], extended[1:, :-1], extended[1:, 1:]], axis=0
    )
    corners = corners.transpose(0, 3, 1, 2, 4)
    return corners.reshape(12, nodes.shape[0] * nodes.shape[1], nodes.shape[3])


def on_device(coefficients, noise_sigma, residual, crack_mask, node_panel):
    n_param = lax.axis_size("param")
    n_row = lax.axis_size("row")
    n_col = lax.axis_size("col")
    tiles = n_row * n_col
    per_block = n_param // tiles
    rows = noise_sigma.shape[1]
    cols = noise_sigma.shape[2]
    elem_rows = rows // EL
    elem_cols = cols // EL
    node_rows, node_cols, comps, width = node_panel.shape
    elements = elem_rows * elem_cols

    shapes = corner_shapes(rows, cols)
    live_rows = jnp.repeat(crack_mask.astype(jnp.float32), 128, axis=1)
    pixel_scale = live_rows[None] / noise_sigma
    design = (
        shapes[:, None, None] * pixel_scale[None, None] * coefficients.astype(jnp.float32)[None]
    ).astype(jnp.bfloat16)
    design = design.reshape(4, 3, CAMS, elem_rows, EL, elem_cols, EL).transpose(3, 5, 0, 1, 2, 4, 6)
    design = design.reshape(elements, 12, CAMS * EL * EL)
    weighted = (pixel_scale * residual).astype(jnp.bfloat16)
    weighted = weighted.reshape(CAMS, elem_rows, EL, elem_cols, EL).transpose(1, 3, 0, 2, 4)
    weighted = weighted.reshape(elements, CAMS * EL * EL)
    gram = jnp.einsum("eip,ejp->eij", design, design, preferred_element_type=jnp.float32)
    proj = jnp.einsum("eip,ep->ei", design, weighted, preferred_element_type=jnp.float32)

    payload = jnp.concatenate([node_panel.reshape(-1).astype(jnp.float32), gram.reshape(-1), proj.reshape(-1)])
    own = exchange_gather(as_lanes(payload, jnp.float32), ("row", "col"))
    own = own.reshape(tiles, -1)
    n_nodes = node_rows * node_cols * comps * width
    n_gram = elements * 144
    own_nodes = own[:, :n_nodes].reshape(n_row, n_col, node_rows, node_cols, comps, width)
    own_nodes = own_nodes.transpose(0, 2, 1, 3, 4, 5).reshape(n_row * node_rows, n_col * node_cols, comps, width)
    grams = own[:, n_nodes : n_nodes + n_gram].reshape(n_row, n_col, elem_rows, elem_cols, 12, 12)
    grams = grams.transpose(0, 2, 1, 3, 4, 5).reshape(-1, 12, 12)
    projs = own[:, n_nodes + n_gram : n_nodes + n_gram + elements * 12]
    projs = projs.reshape(n_row, n_col, elem_rows, elem_cols, 12).transpose(0, 2, 1, 3, 4).reshape(-1, 12)

    places = landing_places(n_param, n_row, n_col, per_block)
    route = []
    for b in range(n_param):
        for t in range(tiles):
            T = b // per_block
            route.append((b * tiles + t, int(places[T, t * per_block + b % per_block]) * tiles + T))
    moved = lax.ppermute(as_lanes(node_panel.reshape(-1), jnp.bfloat16), ("param", "row", "col"), route)
    cross = exchange_gather(moved, "param")
    picks = jnp.asarray(places)[lax.axis_index(("row", "col"))]
    select = (picks[:, None] == jnp.arange(n_param)[None, :]).astype(jnp.bfloat16)
    cross = jnp.einsum("ka,ar->kr", select, cross.reshape(n_param, -1), preferred_element_type=jnp.float32)
    cross = cross.astype(jnp.bfloat16)[:, : node_rows * node_cols * comps * width]
    cross = cross.reshape(n_row, n_col, per_block, node_rows, node_cols, comps, width)
    cross = cross.transpose(0, 3, 1, 4, 5, 2, 6)
    cross = cross.reshape(n_row * node_rows, n_col * node_cols, comps, per_block * width)

    rows_of = element_corners(own_nodes.astype(jnp.bfloat16))
    cols_of = element_corners(cross)
    weighted_rows = jnp.sum(grams.transpose(1, 2, 0)[:, :, :, None] * rows_of.astype(jnp.float32)[:, None], axis=0)
    high = lax.reduce_precision(weighted_rows, exponent_bits=8, mantissa_bits=7)
    low = weighted_rows - high
    stacked = jnp.concatenate([high.astype(jnp.bfloat16), low.astype(jnp.bfloat16)], axis=2)
    product = jnp.einsum("jep,jeq->pq", stacked, cols_of, preferred_element_type=jnp.float32)
    hessian = product[:width] + product[width:]
    proj_high = lax.reduce_precision(projs.T, exponent_bits=8, mantissa_bits=7)
    proj_pair = jnp.stack([proj_high, projs.T - proj_high], axis=2).astype(jnp.bfloat16)
    gradient = jnp.einsum("iep,iek->pk", rows_of, proj_pair, preferred_element_type=jnp.float32).sum(axis=1)
    share = width // tiles
    gradient = lax.dynamic_slice(gradient, (lax.axis_index(("row", "col")) * share,), (share,))
    return (hessian, gradient)


def solution(mesh):
    in_specs = (
        P(None, None, "row", "col"),
        P(None, "row", "col"),
        P(None, "row", "col"),
        P("row", "col"),
        P("row", "col", None, "param"),
    )
    out_specs = (P("param", ("row", "col")), P(("param", "row", "col")))
    return jax.shard_map(
        on_device, mesh=mesh, in_specs=in_specs, out_specs=out_specs, check_vma=False
    )
```

```python
import jax
import jax.numpy as jnp
import numpy as np
from jax import lax
from jax.sharding import PartitionSpec as P

EL = 8
CAMS = 2
LANES = 128
HIGHEST = lax.Precision.HIGHEST

def corner_shapes(rows, cols):
    vertical = ((jnp.arange(rows) % EL).astype(jnp.float32) + 0.5) / EL
    horizontal = ((jnp.arange(cols) % EL).astype(jnp.float32) + 0.5) / EL
    lower = vertical[:, None]
    right = horizontal[None, :]
    return jnp.stack(
        [(1.0 - lower) * (1.0 - right), (1.0 - lower) * right, lower * (1.0 - right), lower * right]
    )


def exchange_gather(piece, axes):
    size = lax.axis_size(axes)
    copies = jnp.broadcast_to(piece[None], (size,) + piece.shape)
    return lax.all_to_all(copies, axes, 0, 0, tiled=False)


def ring_distance(a, b, n):
    d = abs(a - b) % n
    return min(d, n - d)


def landing_places(n_param, n_row, n_col, per_block):
    z_size = n_param // 2
    tiles = n_row * n_col

    def hops(t, j, T, a):
        b = per_block * T + j
        dz = ring_distance(a % z_size, b % z_size, z_size)
        dx = ring_distance(t // n_col, T // n_col, n_row)
        y_from = 2 * ((t % n_col) // 2) + b // z_size
        y_to = 2 * ((T % n_col) // 2) + a // z_size
        return dz + dx + ring_distance(y_from, y_to, 4)

    table = np.zeros((tiles, tiles * per_block), np.int32)
    for T in range(tiles):
        sources = [(t, j) for t in range(tiles) for j in range(per_block)]
        sources.sort(key=lambda s: -(ring_distance(s[0] // n_col, T // n_col, n_row)
                                     + 2 * ring_distance((s[0] % n_col) // 2, (T % n_col) // 2, 2)))
        free = list(range(n_param))
        for t, j in sources:
            place = min(free, key=lambda a: (hops(t, j, T, a), a))
            free.remove(place)
            table[T, t * per_block + j] = place
    return table


def as_lanes(flat, dtype):
    rows = -(-flat.shape[0] // (8 * LANES)) * 8
    flat = jnp.pad(flat.astype(dtype), (0, rows * LANES - flat.shape[0]))
    return flat.reshape(rows, LANES)


def element_corners(nodes):
    extended = jnp.pad(nodes, ((0, 1), (0, 1), (0, 0), (0, 0)))
    corners = jnp.stack(
        [extended[:-1, :-1], extended[:-1, 1:], extended[1:, :-1], extended[1:, 1:]], axis=0
    )
    corners = corners.transpose(0, 3, 1, 2, 4)
    return corners.reshape(12, nodes.shape[0] * nodes.shape[1], nodes.shape[3])


def on_device(coefficients, noise_sigma, residual, crack_mask, node_panel):
    n_param = lax.axis_size("param")
    n_row = lax.axis_size("row")
    n_col = lax.axis_size("col")
    tiles = n_row * n_col
    per_block = n_param // tiles
    rows = noise_sigma.shape[1]
    cols = noise_sigma.shape[2]
    elem_rows = rows // EL
    elem_cols = cols // EL
    node_rows, node_cols, comps, width = node_panel.shape
    elements = elem_rows * elem_cols

    shapes = corner_shapes(rows, cols)
    live_rows = jnp.repeat(crack_mask.astype(jnp.float32), 128, axis=1)
    pixel_scale = live_rows[None] / noise_sigma
    design = (
        shapes[:, None, None] * pixel_scale[None, None] * coefficients.astype(jnp.float32)[None]
    ).astype(jnp.bfloat16)
    design = design.reshape(4, 3, CAMS, elem_rows, EL, elem_cols, EL).transpose(3, 5, 0, 1, 2, 4, 6)
    design = design.reshape(elements, 12, CAMS * EL * EL)
    weighted = (pixel_scale * residual).astype(jnp.bfloat16)
    weighted = weighted.reshape(CAMS, elem_rows, EL, elem_cols, EL).transpose(1, 3, 0, 2, 4)
    weighted = weighted.reshape(elements, CAMS * EL * EL)
    gram = jnp.einsum("eip,ejp->eij", design, design, preferred_element_type=jnp.float32)
    proj = jnp.einsum("eip,ep->ei", design, weighted, preferred_element_type=jnp.float32)

    payload = jnp.concatenate([node_panel.reshape(-1).astype(jnp.float32), gram.reshape(-1), proj.reshape(-1)])
    own = exchange_gather(as_lanes(payload, jnp.float32), ("row", "col"))
    own = own.reshape(tiles, -1)
    n_nodes = node_rows * node_cols * comps * width
    n_gram = elements * 144
    own_nodes = own[:, :n_nodes].reshape(n_row, n_col, node_rows, node_cols, comps, width)
    own_nodes = own_nodes.transpose(0, 2, 1, 3, 4, 5).reshape(n_row * node_rows, n_col * node_cols, comps, width)
    grams = own[:, n_nodes : n_nodes + n_gram].reshape(n_row, n_col, elem_rows, elem_cols, 12, 12)
    grams = grams.transpose(0, 2, 1, 3, 4, 5).reshape(-1, 12, 12)
    projs = own[:, n_nodes + n_gram : n_nodes + n_gram + elements * 12]
    projs = projs.reshape(n_row, n_col, elem_rows, elem_cols, 12).transpose(0, 2, 1, 3, 4).reshape(-1, 12)

    places = landing_places(n_param, n_row, n_col, per_block)
    route = []
    for b in range(n_param):
        for t in range(tiles):
            T = b // per_block
            route.append((b * tiles + t, int(places[T, t * per_block + b % per_block]) * tiles + T))
    moved = lax.ppermute(as_lanes(node_panel.reshape(-1), jnp.bfloat16), ("param", "row", "col"), route)
    cross = exchange_gather(moved, "param")
    picks = jnp.asarray(places)[lax.axis_index(("row", "col"))]
    select = (picks[:, None] == jnp.arange(n_param)[None, :]).astype(jnp.bfloat16)
    cross = jnp.einsum("ka,ar->kr", select, cross.reshape(n_param, -1), preferred_element_type=jnp.float32)
    cross = cross.astype(jnp.bfloat16)[:, : node_rows * node_cols * comps * width]
    cross = cross.reshape(n_row, n_col, per_block, node_rows, node_cols, comps, width)
    cross = cross.transpose(0, 3, 1, 4, 5, 2, 6)
    cross = cross.reshape(n_row * node_rows, n_col * node_cols, comps, per_block * width)

    rows_of = element_corners(own_nodes.astype(jnp.bfloat16))
    cols_of = element_corners(cross)
    weighted_rows = jnp.sum(grams.transpose(1, 2, 0)[:, :, :, None] * rows_of.astype(jnp.float32)[:, None], axis=0)
    high = lax.reduce_precision(weighted_rows, exponent_bits=8, mantissa_bits=7)
    low = weighted_rows - high
    stacked = jnp.concatenate([high.astype(jnp.bfloat16), low.astype(jnp.bfloat16)], axis=0)
    paired = jnp.concatenate([cols_of, cols_of], axis=0)
    hessian = jnp.einsum("jep,jeq->pq", stacked, paired, preferred_element_type=jnp.float32)
    gradient = jnp.einsum("iep,ie->p", rows_of.astype(jnp.float32), projs.T, precision=HIGHEST)
    share = width // tiles
    gradient = lax.dynamic_slice(gradient, (lax.axis_index(("row", "col")) * share,), (share,))
    return (hessian, gradient)


def solution(mesh):
    in_specs = (
        P(None, None, "row", "col"),
        P(None, "row", "col"),
        P(None, "row", "col"),
        P("row", "col"),
        P("row", "col", None, "param"),
    )
    out_specs = (P("param", ("row", "col")), P(("param", "row", "col")))
    return jax.shard_map(
        on_device, mesh=mesh, in_specs=in_specs, out_specs=out_specs, check_vma=False
    )
```
